768 devices in a mesh: ctx: 32 (over z_hi, y, core), tp: 24 (over z_lo, x).
Axes of the slice: x: 4, y: 8, z: 12 (z_hi: 2, z_lo: 6; z = z_hi * 6 + z_lo), core: 2. Of those that a mesh axis runs over, the one named last changes fastest.
Arguments:
- queries: bfloat16 [4096, 3072], P('ctx', 'tp'), may hold values from -40 to 40
- keys: bfloat16 [4096, 768], P('ctx'), may hold values from -6 to 6
- values: bfloat16 [4096, 768], P('ctx'), may hold values from -6 to 6
- roles: int32 [4096], P('ctx'), may hold values from 0 to 15
- role_table: float32 [24, 16, 16], P('tp'), may hold values from -4 to 4
- block_mask: int32 [32, 32], replicated, may hold values 0 or 1
- d_out: bfloat16 [4096, 3072], P('ctx', 'tp'), may hold values from -6 to 6
Outputs:
- attended: bfloat16 [4096, 3072], P('ctx', 'tp')
- d_queries: bfloat16 [4096, 3072], P('ctx', 'tp')
- d_keys: bfloat16 [4096, 768], P('ctx')
- d_values: bfloat16 [4096, 768], P('ctx')
The draws below stay inside these ranges and needn't reach their ends.
All inputs are finite; a program needn't handle non-finite values.
Results may differ from the reference program's by a relative error of at most 0.034.
Values may be sent and summed in bfloat16 or wider, within the bound.
No kernel may reach another device: no remote copies, remote signals or barrier semaphores. Data moves between devices by JAX's collectives and lax.ppermute only.
A program may use at most 32 MiB of HBM per device.

```python
import math
import jax
import jax.numpy as jnp
from jax import lax

HS = 128
QH = 24
GROUP = 4
KVH = 6
ROLES = 16
BLK = 128
L = 4096
NBLK = 32


def draw_pair(key):
    query_key = jax.random.fold_in(key, 11)
    other_key = jax.random.fold_in(key, 12)
    query = jnp.clip(jax.random.normal(query_key, (L, QH * HS), jnp.float32), -6.0, 6.0)
    base = jnp.clip(jax.random.normal(other_key, (L, KVH * HS), jnp.float32), -6.0, 6.0)
    return (query, base)


def draw_queries(key, part):
    return draw_pair(key)[0].astype(jnp.bfloat16)


def draw_keys(key, part):
    return draw_pair(key)[1].astype(jnp.bfloat16)


def set_ends(result, rng, low, high):
    extent = result.shape
    index_at = [jax.random.randint(jax.random.fold_in(rng, axis), (), 0, extent[axis]) for axis in range(len(extent))]
    result = result.at[tuple(index_at)].set(low)
    longest = extent.index(max(extent))
    index_at[longest] = (index_at[longest] + 1) % extent[longest]
    return result.at[tuple(index_at)].set(high)


def steps_of(key, shape, pieces, low, largest):
    def one(dim, shards_of):
        steps = jax.random.uniform(jax.random.fold_in(jax.random.fold_in(key, 6), dim), (shards_of,), jnp.float32, low / len(pieces), largest / len(pieces))
        return jnp.repeat(jnp.exp(steps), shape[dim] // shards_of).reshape((-1,) + (1,) * (len(shape) - dim - 1))

    level = one(*pieces[0])
    for cut in pieces[1:]:
        level = level * one(*cut)
    return level


def gaussian(stream_key, shape, scale, bound, split=(), kind=jnp.bfloat16):
    array = scale * jax.random.normal(stream_key, shape, jnp.float32)
    if split:
        array = array * steps_of(stream_key, shape, split, -0.22, 0.18)
    return jnp.clip(array, -bound, bound).astype(kind)


def setup_inputs(seed: int = 0) -> dict:
    arg_keys = jax.random.split(jax.random.key(seed), 8)
    return {
        "queries": draw_queries(jax.random.fold_in(arg_keys[7], 71), 0),
        "keys": draw_keys(jax.random.fold_in(arg_keys[7], 71), 0),
        "values": gaussian(arg_keys[2], (L, KVH * HS), 1.0, 6.0, ((0, 32),)),
        "roles": set_ends(jax.random.randint(arg_keys[3], (L,), 0, ROLES), jax.random.fold_in(arg_keys[3], 1), 0, ROLES - 1).astype(jnp.int32),
        "role_table": gaussian(arg_keys[4], (QH, ROLES, ROLES), 1.0, 4.0, ((0, 24),), jnp.float32),
        "block_mask": set_ends((jax.random.randint(arg_keys[5], (NBLK, NBLK), 0, 4) < 3).astype(jnp.int32), jax.random.fold_in(arg_keys[5], 1), 0, 1),
        "d_out": gaussian(arg_keys[6], (L, QH * HS), 1.0, 6.0, ((0, 32), (1, 24))),
    }


def reference(queries, keys, values, roles, role_table, block_mask, d_out):
    scale = 1.0 / math.sqrt(HS)
    position = jnp.arange(L)
    blocks = position // BLK
    allowed = (position[None, :] <= position[:, None]) & ((block_mask[blocks[:, None], blocks[None, :]] == 1) | (blocks[:, None] == blocks[None, :]))
    query_heads = queries.reshape(L, QH, HS).transpose(1, 0, 2)
    grad_heads = d_out.reshape(L, QH, HS).transpose(1, 0, 2)
    key_heads = keys.reshape(L, KVH, HS).transpose(1, 0, 2)
    value_heads = values.reshape(L, KVH, HS).transpose(1, 0, 2)

    def one_head(inputs):
        query, grad, table, head = inputs
        key = key_heads[head // GROUP]
        value = value_heads[head // GROUP]
        score = jnp.dot(query, key.T, preferred_element_type=jnp.float32) * scale + table[roles[:, None], roles[None, :]]
        score = jnp.where(allowed, score, jnp.float32(-1e+30))
        top = lax.optimization_barrier(jnp.max(score, axis=1))
        expo = jnp.where(allowed, jnp.exp(score - top[:, None]), jnp.float32(0.0))
        total = lax.optimization_barrier(jnp.sum(expo, axis=1))
        output = jnp.dot(expo.astype(jnp.bfloat16), value, preferred_element_type=jnp.float32) / total[:, None]
        output = output.astype(jnp.bfloat16)
        lse = top + jnp.log(total)
        prob = jnp.where(allowed, jnp.exp(score - lse[:, None]), jnp.float32(0.0))
        dprob = jnp.dot(grad, value.T, preferred_element_type=jnp.float32)
        delta = lax.optimization_barrier(jnp.sum(grad.astype(jnp.float32) * output.astype(jnp.float32), axis=1))
        dscore = (prob * (dprob - delta[:, None])).astype(jnp.bfloat16)
        d_query = (jnp.dot(dscore, key, preferred_element_type=jnp.float32) * scale).astype(jnp.bfloat16)
        d_key = jnp.dot(dscore.T, query, preferred_element_type=jnp.float32) * scale
        d_value = jnp.dot(prob.astype(jnp.bfloat16).T, grad, preferred_element_type=jnp.float32)
        return (output, d_query, d_key, d_value)
    outputs, d_query, d_key, d_value = lax.map(one_head, (query_heads, grad_heads, role_table, jnp.arange(QH)))
    attended = outputs.transpose(1, 0, 2).reshape(L, QH * HS)
    d_queries = d_query.transpose(1, 0, 2).reshape(L, QH * HS)
    d_keys = d_key.reshape(KVH, GROUP, L, HS).sum(axis=1).transpose(1, 0, 2).reshape(L, KVH * HS).astype(jnp.bfloat16)
    d_values = d_value.reshape(KVH, GROUP, L, HS).sum(axis=1).transpose(1, 0, 2).reshape(L, KVH * HS).astype(jnp.bfloat16)
    return (attended, d_queries, d_keys, d_values)
```

```python
import math

import jax
import jax.numpy as jnp
import numpy as np
from jax import lax
from jax.sharding import Mesh
from jax.sharding import PartitionSpec as P

HS = 128
GROUP = 4
BLK = 128
NEG = -1e30
HI = lax.Precision.HIGHEST


def on_device(queries, keys, values, roles, role_table, block_mask, d_out):
    rows = queries.shape[0]
    role_count = role_table.shape[1]
    scale = 1.0 / math.sqrt(HS)
    ctx_index = lax.axis_index("ctx")
    group = lax.axis_index("g")
    own_keys = lax.dynamic_slice_in_dim(keys, group * HS, HS, 1)
    own_values = lax.dynamic_slice_in_dim(values, group * HS, HS, 1)
    table = role_table[0]

    role_onehot = (roles[:, None] == jnp.arange(role_count)[None, :]).astype(jnp.float32)
    role_slot = jnp.pad(role_onehot, ((0, 0), (0, HS - role_count))).astype(jnp.bfloat16)
    packed = jnp.stack([own_keys, own_values, queries, d_out, role_slot], axis=1)
    every = lax.all_gather(packed, "ctx", axis=0, tiled=True)
    total_rows = every.shape[0]
    all_keys = every[:, 0]
    all_values = every[:, 1]
    all_queries = every[:, 2]
    all_grads = every[:, 3]
    all_onehot = every[:, 4, :role_count].astype(jnp.float32)

    pos = jnp.arange(total_rows)
    own_pos = ctx_index * rows + jnp.arange(rows)
    mask_f = block_mask.astype(jnp.float32)
    all_block = (pos[:, None] // BLK == jnp.arange(block_mask.shape[0])[None, :]).astype(jnp.float32)
    own_block = (own_pos[:, None] // BLK == jnp.arange(block_mask.shape[0])[None, :]).astype(jnp.float32)

    q_open = jnp.dot(jnp.dot(own_block, mask_f, precision=HI), all_block.T, precision=HI) > 0.5
    q_allowed = (pos[None, :] <= own_pos[:, None]) & (
        q_open | (pos[None, :] // BLK == own_pos[:, None] // BLK)
    )
    q_bias = jnp.dot(jnp.dot(role_onehot, table, precision=HI), all_onehot.T, precision=HI)
    score = jnp.dot(queries, all_keys.T, preferred_element_type=jnp.float32) * scale + q_bias
    score = jnp.where(q_allowed, score, jnp.float32(NEG))
    top = jnp.max(score, axis=-1)
    expo = jnp.where(q_allowed, jnp.exp(score - top[:, None]), jnp.float32(0.0))
    total = jnp.sum(expo, axis=-1)
    out = jnp.dot(expo.astype(jnp.bfloat16), all_values, preferred_element_type=jnp.float32)
    out = (out / total[:, None]).astype(jnp.bfloat16)
    lse = top + jnp.log(total)
    delta = jnp.sum(d_out.astype(jnp.float32) * out.astype(jnp.float32), axis=-1)
    prob = jnp.where(q_allowed, jnp.exp(score - lse[:, None]), jnp.float32(0.0))
    dprob = jnp.dot(d_out, all_values.T, preferred_element_type=jnp.float32)
    dscore = (prob * (dprob - delta[:, None])).astype(jnp.bfloat16)
    d_query = jnp.dot(dscore, all_keys, preferred_element_type=jnp.float32) * scale

    stats = lax.all_gather(jnp.stack([lse, delta], axis=0), "ctx", axis=1, tiled=True)
    all_lse = stats[0]
    all_delta = stats[1]

    k_open = jnp.dot(jnp.dot(all_block, mask_f, precision=HI), own_block.T, precision=HI) > 0.5
    k_allowed = (own_pos[None, :] <= pos[:, None]) & (
        k_open | (own_pos[None, :] // BLK == pos[:, None] // BLK)
    )
    k_bias = jnp.dot(all_onehot, jnp.dot(table, role_onehot.T, precision=HI), precision=HI)
    score_t = jnp.dot(all_queries, own_keys.T, preferred_element_type=jnp.float32) * scale + k_bias
    prob_t = jnp.where(k_allowed, jnp.exp(score_t - all_lse[:, None]), jnp.float32(0.0))
    dprob_t = jnp.dot(all_grads, own_values.T, preferred_element_type=jnp.float32)
    dscore_t = (prob_t * (dprob_t - all_delta[:, None])).astype(jnp.bfloat16)
    d_key = jnp.dot(dscore_t.T, all_queries, preferred_element_type=jnp.float32) * scale
    d_value = jnp.dot(prob_t.astype(jnp.bfloat16).T, all_grads, preferred_element_type=jnp.float32)

    kv_grad = lax.psum(jnp.stack([d_key, d_value], axis=0), "x").astype(jnp.bfloat16)
    kv_all = lax.all_gather(kv_grad, "g", axis=2, tiled=True)
    return (out, d_query.astype(jnp.bfloat16), kv_all[0], kv_all[1])


def solution(mesh):
    ctx_size = mesh.shape["ctx"]
    tp_size = mesh.shape["tp"]
    devices = np.asarray(mesh.devices).reshape(ctx_size, tp_size // GROUP, GROUP)
    inner = Mesh(devices, ("ctx", "g", "x"))
    heads = ("g", "x")
    return jax.shard_map(
        on_device,
        mesh=inner,
        in_specs=(
            P("ctx", heads),
            P("ctx", None),
            P("ctx", None),
            P("ctx"),
            P(heads, None, None),
            P(),
            P("ctx", heads),
        ),
        out_specs=(P("ctx", heads), P("ctx", heads), P("ctx", None), P("ctx", None)),
        check_vma=False,
    )
```

```python
import math

import jax
import jax.numpy as jnp
import numpy as np
from jax import lax
from jax.sharding import Mesh
from jax.sharding import PartitionSpec as P

HS = 128
GROUP = 4
BLK = 128
NEG = -1e30
HI = lax.Precision.HIGHEST


def xor_pairs(count, bit):
    return [(i, i ^ bit) for i in range(count)]


def xor_gather(block, axis):
    count = lax.axis_size(axis)
    me = lax.axis_index(axis)
    held = block[None]
    bit = 1
    while bit < count:
        held = jnp.concatenate([held, lax.ppermute(held, axis, xor_pairs(count, bit))], axis=0)
        bit *= 2
    return jnp.take(held, me ^ jnp.arange(count), axis=0)


def xor_sum(value, axis):
    count = lax.axis_size(axis)
    bit = 1
    while bit < count:
        value = value + lax.ppermute(value, axis, xor_pairs(count, bit))
        bit *= 2
    return value


def bruck_gather(block, axis):
    count = lax.axis_size(axis)
    me = lax.axis_index(axis)
    held = block[None]
    step = 1
    while step < count:
        part = held[: min(step, count - step)]
        pairs = [(i, (i - step) % count) for i in range(count)]
        held = jnp.concatenate([held, lax.ppermute(part, axis, pairs)], axis=0)
        step *= 2
    return jnp.take(held, (jnp.arange(count) - me) % count, axis=0)


def on_device(queries, keys, values, roles, role_table, block_mask, d_out):
    rows = queries.shape[0]
    role_count = role_table.shape[1]
    scale = 1.0 / math.sqrt(HS)
    ctx_index = lax.axis_index("ctx")
    group = lax.axis_index("g")
    own_keys = lax.dynamic_slice_in_dim(keys, group * HS, HS, 1)
    own_values = lax.dynamic_slice_in_dim(values, group * HS, HS, 1)
    table = role_table[0]

    role_onehot = (roles[:, None] == jnp.arange(role_count)[None, :]).astype(jnp.float32)
    role_slot = jnp.pad(role_onehot, ((0, 0), (0, HS - role_count))).astype(jnp.bfloat16)
    packed = jnp.stack([own_keys, own_values, queries, d_out, role_slot], axis=1)
    every = lax.all_gather(packed, "ctx", axis=0, tiled=True)
    total_rows = every.shape[0]
    all_keys = every[:, 0]
    all_values = every[:, 1]
    all_queries = every[:, 2]
    all_grads = every[:, 3]
    all_onehot = every[:, 4, :role_count].astype(jnp.float32)

    pos = jnp.arange(total_rows)
    own_pos = ctx_index * rows + jnp.arange(rows)
    mask_f = block_mask.astype(jnp.float32)
    all_block = (pos[:, None] // BLK == jnp.arange(block_mask.shape[0])[None, :]).astype(jnp.float32)
    own_block = (own_pos[:, None] // BLK == jnp.arange(block_mask.shape[0])[None, :]).astype(jnp.float32)

    q_open = jnp.dot(jnp.dot(own_block, mask_f, precision=HI), all_block.T, precision=HI) > 0.5
    q_allowed = (pos[None, :] <= own_pos[:, None]) & (
        q_open | (pos[None, :] // BLK == own_pos[:, None] // BLK)
    )
    q_bias = jnp.dot(jnp.dot(role_onehot, table, precision=HI), all_onehot.T, precision=HI)
    score = jnp.dot(queries, all_keys.T, preferred_element_type=jnp.float32) * scale + q_bias
    score = jnp.where(q_allowed, score, jnp.float32(NEG))
    top = jnp.max(score, axis=-1)
    expo = jnp.where(q_allowed, jnp.exp(score - top[:, None]), jnp.float32(0.0))
    total = jnp.sum(expo, axis=-1)
    out = jnp.dot(expo.astype(jnp.bfloat16), all_values, preferred_element_type=jnp.float32)
    out = (out / total[:, None]).astype(jnp.bfloat16)
    lse = top + jnp.log(total)
    delta = jnp.sum(d_out.astype(jnp.float32) * out.astype(jnp.float32), axis=-1)
    prob = jnp.where(q_allowed, jnp.exp(score - lse[:, None]), jnp.float32(0.0))
    dprob = jnp.dot(d_out, all_values.T, preferred_element_type=jnp.float32)
    dscore = (prob * (dprob - delta[:, None])).astype(jnp.bfloat16)
    d_query = jnp.dot(dscore, all_keys, preferred_element_type=jnp.float32) * scale

    stats = xor_gather(jnp.stack([lse, delta], axis=0), "ctx")
    all_lse = stats[:, 0].reshape(total_rows)
    all_delta = stats[:, 1].reshape(total_rows)

    k_open = jnp.dot(jnp.dot(all_block, mask_f, precision=HI), own_block.T, precision=HI) > 0.5
    k_allowed = (own_pos[None, :] <= pos[:, None]) & (
        k_open | (own_pos[None, :] // BLK == pos[:, None] // BLK)
    )
    k_bias = jnp.dot(all_onehot, jnp.dot(table, role_onehot.T, precision=HI), precision=HI)
    score_t = jnp.dot(all_queries, own_keys.T, preferred_element_type=jnp.float32) * scale + k_bias
    prob_t = jnp.where(k_allowed, jnp.exp(score_t - all_lse[:, None]), jnp.float32(0.0))
    dprob_t = jnp.dot(all_grads, own_values.T, preferred_element_type=jnp.float32)
    dscore_t = (prob_t * (dprob_t - all_delta[:, None])).astype(jnp.bfloat16)
    d_key = jnp.dot(dscore_t.T, all_queries, preferred_element_type=jnp.float32) * scale
    d_value = jnp.dot(prob_t.astype(jnp.bfloat16).T, all_grads, preferred_element_type=jnp.float32)

    kv_grad = xor_sum(jnp.stack([d_key, d_value], axis=0), "x").astype(jnp.bfloat16)
    kv_all = bruck_gather(kv_grad, "g")
    kv_all = kv_all.transpose(1, 2, 0, 3).reshape(2, rows, -1)
    return (out, d_query.astype(jnp.bfloat16), kv_all[0], kv_all[1])


def solution(mesh):
    ctx_size = mesh.shape["ctx"]
    tp_size = mesh.shape["tp"]
    devices = np.asarray(mesh.devices).reshape(ctx_size, tp_size // GROUP, GROUP)
    inner = Mesh(devices, ("ctx", "g", "x"))
    heads = ("g", "x")
    return jax.shard_map(
        on_device,
        mesh=inner,
        in_specs=(
            P("ctx", heads),
            P("ctx", None),
            P("ctx", None),
            P("ctx"),
            P(heads, None, None),
            P(),
            P("ctx", heads),
        ),
        out_specs=(P("ctx", heads), P("ctx", heads), P("ctx", None), P("ctx", None)),
        check_vma=False,
    )
```

```python
import math

import jax
import jax.numpy as jnp
import numpy as np
from jax import lax
from jax.sharding import Mesh
from jax.sharding import PartitionSpec as P

HS = 128
GROUP = 4
BLK = 128
NEG = -1e30
HI = lax.Precision.HIGHEST


def xor_pairs(count, bit):
    return [(i, i ^ bit) for i in range(count)]


def xor_gather(block, axis):
    count = lax.axis_size(axis)
    me = lax.axis_index(axis)
    held = block[None]
    bit = 1
    while bit < count:
        held = jnp.concatenate([held, lax.ppermute(held, axis, xor_pairs(count, bit))], axis=0)
        bit *= 2
    return jnp.take(held, me ^ jnp.arange(count), axis=0)


def xor_sum(value, axis):
    count = lax.axis_size(axis)
    bit = 1
    while bit < count:
        value = value + lax.ppermute(value, axis, xor_pairs(count, bit))
        bit *= 2
    return value


def bruck_gather(block, axis):
    count = lax.axis_size(axis)
    me = lax.axis_index(axis)
    held = block[None]
    step = 1
    while step < count:
        part = held[: min(step, count - step)]
        pairs = [(i, (i - step) % count) for i in range(count)]
        held = jnp.concatenate([held, lax.ppermute(part, axis, pairs)], axis=0)
        step *= 2
    return jnp.take(held, (jnp.arange(count) - me) % count, axis=0)


def shift_pairs(count, step):
    return [(i, (i + step) % count) for i in range(count)]


def gather_ctx(block):
    zh = lax.axis_index("zh")
    y = lax.axis_index("y")
    core = lax.axis_index("core")
    ny = lax.axis_size("y")
    ncore = lax.axis_size("core")
    nz = lax.axis_size("zh")

    def index_of(z, yy, cc):
        return (z * ny + yy) * ncore + cc

    held = [block[None], lax.ppermute(block[None], "zh", xor_pairs(nz, 1))]
    chip = jnp.concatenate(held, axis=0)
    blocks = [chip]
    owners = [jnp.stack([index_of(zh, y, core), index_of(1 - zh, y, core)])]
    left = chip
    right = chip
    for step in range(1, ny // 2 + 1):
        left = lax.ppermute(left, "y", shift_pairs(ny, 1))
        blocks.append(left)
        yy = (y - step) % ny
        owners.append(jnp.stack([index_of(zh, yy, core), index_of(1 - zh, yy, core)]))
        if step < ny - step:
            right = lax.ppermute(right, "y", shift_pairs(ny, -1))
            blocks.append(right)
            yy = (y + step) % ny
            owners.append(jnp.stack([index_of(zh, yy, core), index_of(1 - zh, yy, core)]))
    mine = jnp.concatenate(blocks, axis=0)
    owner = jnp.concatenate(owners, axis=0)
    other = lax.ppermute(mine, "core", xor_pairs(ncore, 1))
    every = jnp.concatenate([mine, other], axis=0)
    owner = jnp.concatenate([owner, owner - core + (1 - core)], axis=0)
    return every, owner


def on_device(queries, keys, values, roles, role_table, block_mask, d_out):
    rows = queries.shape[0]
    role_count = role_table.shape[1]
    scale = 1.0 / math.sqrt(HS)
    ctx_index = (lax.axis_index("zh") * lax.axis_size("y") + lax.axis_index("y")) * lax.axis_size(
        "core"
    ) + lax.axis_index("core")
    group = lax.axis_index("g")
    own_keys = lax.dynamic_slice_in_dim(keys, group * HS, HS, 1)
    own_values = lax.dynamic_slice_in_dim(values, group * HS, HS, 1)
    table = role_table[0]

    role_onehot = (roles[:, None] == jnp.arange(role_count)[None, :]).astype(jnp.float32)
    role_slot = jnp.pad(role_onehot, ((0, 0), (0, HS - role_count))).astype(jnp.bfloat16)
    packed = jnp.stack([own_keys, own_values, queries, d_out, role_slot], axis=1)
    every, owner = gather_ctx(packed)
    every = every.reshape((-1,) + packed.shape[1:])
    total_rows = every.shape[0]
    all_keys = every[:, 0]
    all_values = every[:, 1]
    all_queries = every[:, 2]
    all_grads = every[:, 3]
    all_onehot = every[:, 4, :role_count].astype(jnp.float32)

    pos = (owner[:, None] * rows + jnp.arange(rows)[None, :]).reshape(total_rows)
    own_pos = ctx_index * rows + jnp.arange(rows)
    mask_f = block_mask.astype(jnp.float32)
    all_block = (pos[:, None] // BLK == jnp.arange(block_mask.shape[0])[None, :]).astype(jnp.float32)
    own_block = (own_pos[:, None] // BLK == jnp.arange(block_mask.shape[0])[None, :]).astype(jnp.float32)

    q_open = jnp.dot(jnp.dot(own_block, mask_f, precision=HI), all_block.T, precision=HI) > 0.5
    q_allowed = (pos[None, :] <= own_pos[:, None]) & (
        q_open | (pos[None, :] // BLK == own_pos[:, None] // BLK)
    )
    q_bias = jnp.dot(jnp.dot(role_onehot, table, precision=HI), all_onehot.T, precision=HI)
    score = jnp.dot(queries, all_keys.T, preferred_element_type=jnp.float32) * scale + q_bias
    score = jnp.where(q_allowed, score, jnp.float32(NEG))
    top = jnp.max(score, axis=-1)
    expo = jnp.where(q_allowed, jnp.exp(score - top[:, None]), jnp.float32(0.0))
    total = jnp.sum(expo, axis=-1)
    out = jnp.dot(expo.astype(jnp.bfloat16), all_values, preferred_element_type=jnp.float32)
    out = (out / total[:, None]).astype(jnp.bfloat16)
    lse = top + jnp.log(total)
    delta = jnp.sum(d_out.astype(jnp.float32) * out.astype(jnp.float32), axis=-1)
    prob = jnp.where(q_allowed, jnp.exp(score - lse[:, None]), jnp.float32(0.0))
    dprob = jnp.dot(d_out, all_values.T, preferred_element_type=jnp.float32)
    dscore = (prob * (dprob - delta[:, None])).astype(jnp.bfloat16)
    d_query = jnp.dot(dscore, all_keys, preferred_element_type=jnp.float32) * scale

    stats = jnp.take(xor_gather(jnp.stack([lse, delta], axis=0), ("zh", "y", "core")), owner, axis=0)
    all_lse = stats[:, 0].reshape(total_rows)
    all_delta = stats[:, 1].reshape(total_rows)

    k_open = jnp.dot(jnp.dot(all_block, mask_f, precision=HI), own_block.T, precision=HI) > 0.5
    k_allowed = (own_pos[None, :] <= pos[:, None]) & (
        k_open | (own_pos[None, :] // BLK == pos[:, None] // BLK)
    )
    k_bias = jnp.dot(all_onehot, jnp.dot(table, role_onehot.T, precision=HI), precision=HI)
    score_t = jnp.dot(all_queries, own_keys.T, preferred_element_type=jnp.float32) * scale + k_bias
    prob_t = jnp.where(k_allowed, jnp.exp(score_t - all_lse[:, None]), jnp.float32(0.0))
    dprob_t = jnp.dot(all_grads, own_values.T, preferred_element_type=jnp.float32)
    dscore_t = (prob_t * (dprob_t - all_delta[:, None])).astype(jnp.bfloat16)
    d_key = jnp.dot(dscore_t.T, all_queries, preferred_element_type=jnp.float32) * scale
    d_value = jnp.dot(prob_t.astype(jnp.bfloat16).T, all_grads, preferred_element_type=jnp.float32)

    kv_grad = xor_sum(jnp.stack([d_key, d_value], axis=0), "x").astype(jnp.bfloat16)
    kv_all = bruck_gather(kv_grad, "g")
    kv_all = kv_all.transpose(1, 2, 0, 3).reshape(2, rows, -1)
    return (out, d_query.astype(jnp.bfloat16), kv_all[0], kv_all[1])


def solution(mesh):
    ctx_size = mesh.shape["ctx"]
    tp_size = mesh.shape["tp"]
    devices = np.asarray(mesh.devices).reshape(ctx_size, tp_size // GROUP, GROUP)
    inner = Mesh(devices.reshape(2, ctx_size // 4, 2, tp_size // GROUP, GROUP), ("zh", "y", "core", "g", "x"))
    heads = ("g", "x")
    seq = ("zh", "y", "core")
    return jax.shard_map(
        on_device,
        mesh=inner,
        in_specs=(
            P(seq, heads),
            P(seq, None),
            P(seq, None),
            P(seq),
            P(heads, None, None),
            P(),
            P(seq, heads),
        ),
        out_specs=(P(seq, heads), P(seq, heads), P(seq, None), P(seq, None)),
        check_vma=False,
    )
```

```python
import math

import jax
import jax.numpy as jnp
import numpy as np
from jax import lax
from jax.sharding import Mesh
from jax.sharding import PartitionSpec as P

HS = 128
GROUP = 4
BLK = 128
NEG = -1e30
HI = lax.Precision.HIGHEST


def xor_pairs(count, bit):
    return [(i, i ^ bit) for i in range(count)]


def xor_gather(block, axis):
    count = lax.axis_size(axis)
    me = lax.axis_index(axis)
    held = block[None]
    bit = 1
    while bit < count:
        held = jnp.concatenate([held, lax.ppermute(held, axis, xor_pairs(count, bit))], axis=0)
        bit *= 2
    return jnp.take(held, me ^ jnp.arange(count), axis=0)


def xor_sum(value, axis):
    count = lax.axis_size(axis)
    bit = 1
    while bit < count:
        value = value + lax.ppermute(value, axis, xor_pairs(count, bit))
        bit *= 2
    return value


def bruck_gather(block, axis):
    count = lax.axis_size(axis)
    me = lax.axis_index(axis)
    held = block[None]
    step = 1
    while step < count:
        part = held[: min(step, count - step)]
        pairs = [(i, (i - step) % count) for i in range(count)]
        held = jnp.concatenate([held, lax.ppermute(part, axis, pairs)], axis=0)
        step *= 2
    return jnp.take(held, (jnp.arange(count) - me) % count, axis=0)


def shift_pairs(count, step):
    return [(i, (i + step) % count) for i in range(count)]


def gather_ctx(block):
    zh = lax.axis_index("zh")
    y = lax.axis_index("y")
    core = lax.axis_index("core")
    ny = lax.axis_size("y")
    ncore = lax.axis_size("core")
    nz = lax.axis_size("zh")

    def index_of(z, yy, cc):
        return (z * ny + yy) * ncore + cc

    held = [block[None], lax.ppermute(block[None], "zh", xor_pairs(nz, 1))]
    chip = jnp.concatenate(held, axis=0)
    blocks = [chip]
    owners = [jnp.stack([index_of(zh, y, core), index_of(1 - zh, y, core)])]
    left = chip
    right = chip
    for step in range(1, ny // 2 + 1):
        left = lax.ppermute(left, "y", shift_pairs(ny, 1))
        blocks.append(left)
        yy = (y - step) % ny
        owners.append(jnp.stack([index_of(zh, yy, core), index_of(1 - zh, yy, core)]))
        if step < ny - step:
            right = lax.ppermute(right, "y", shift_pairs(ny, -1))
            blocks.append(right)
            yy = (y + step) % ny
            owners.append(jnp.stack([index_of(zh, yy, core), index_of(1 - zh, yy, core)]))
    mine = jnp.concatenate(blocks, axis=0)
    owner = jnp.concatenate(owners, axis=0)
    other = lax.ppermute(mine, "core", xor_pairs(ncore, 1))
    every = jnp.concatenate([mine, other], axis=0)
    owner = jnp.concatenate([owner, owner - core + (1 - core)], axis=0)
    return every, owner


def shifted_all(value, axis):
    count = lax.axis_size(axis)
    me = lax.axis_index(axis)
    parts = [value] + [lax.ppermute(value, axis, shift_pairs(count, s)) for s in range(1, count)]
    return jnp.take(jnp.stack(parts), (me - jnp.arange(count)) % count, axis=0)


def on_device(queries, keys, values, roles, role_table, block_mask, d_out):
    rows = queries.shape[0]
    role_count = role_table.shape[1]
    scale = 1.0 / math.sqrt(HS)
    ctx_index = (lax.axis_index("zh") * lax.axis_size("y") + lax.axis_index("y")) * lax.axis_size(
        "core"
    ) + lax.axis_index("core")
    group = lax.axis_index("g")
    own_keys = lax.dynamic_slice_in_dim(keys, group * HS, HS, 1)
    own_values = lax.dynamic_slice_in_dim(values, group * HS, HS, 1)
    table = role_table[0]

    role_onehot = (roles[:, None] == jnp.arange(role_count)[None, :]).astype(jnp.float32)
    role_rows = jnp.zeros((16, rows), jnp.bfloat16).at[0].set(roles.astype(jnp.bfloat16))
    packed = jnp.concatenate([own_keys, own_values, queries, d_out, role_rows], axis=0)
    every, owner = gather_ctx(packed)
    total_rows = every.shape[0] * rows
    all_keys = every[:, 0:rows].reshape(total_rows, HS)
    all_values = every[:, rows : 2 * rows].reshape(total_rows, HS)
    all_queries = every[:, 2 * rows : 3 * rows].reshape(total_rows, HS)
    all_grads = every[:, 3 * rows : 4 * rows].reshape(total_rows, HS)
    all_roles = every[:, 4 * rows].reshape(total_rows).astype(jnp.int32)
    all_onehot = (all_roles[:, None] == jnp.arange(role_count)[None, :]).astype(jnp.float32)

    pos = (owner[:, None] * rows + jnp.arange(rows)[None, :]).reshape(total_rows)
    own_pos = ctx_index * rows + jnp.arange(rows)
    mask_f = block_mask.astype(jnp.float32)
    all_block = (pos[:, None] // BLK == jnp.arange(block_mask.shape[0])[None, :]).astype(jnp.float32)
    own_block = (own_pos[:, None] // BLK == jnp.arange(block_mask.shape[0])[None, :]).astype(jnp.float32)

    q_open = jnp.dot(jnp.dot(own_block, mask_f, precision=HI), all_block.T, precision=HI) > 0.5
    q_allowed = (pos[None, :] <= own_pos[:, None]) & (
        q_open | (pos[None, :] // BLK == own_pos[:, None] // BLK)
    )
    q_bias = jnp.dot(jnp.dot(role_onehot, table, precision=HI), all_onehot.T, precision=HI)
    score = jnp.dot(queries, all_keys.T, preferred_element_type=jnp.float32) * scale + q_bias
    score = jnp.where(q_allowed, score, jnp.float32(NEG))
    top = jnp.max(score, axis=-1)
    expo = jnp.where(q_allowed, jnp.exp(score - top[:, None]), jnp.float32(0.0))
    total = jnp.sum(expo, axis=-1)
    out = jnp.dot(expo.astype(jnp.bfloat16), all_values, preferred_element_type=jnp.float32)
    out = (out / total[:, None]).astype(jnp.bfloat16)
    lse = top + jnp.log(total)
    delta = jnp.sum(d_out.astype(jnp.float32) * out.astype(jnp.float32), axis=-1)
    prob = jnp.where(q_allowed, jnp.exp(score - lse[:, None]), jnp.float32(0.0))
    dprob = jnp.dot(d_out, all_values.T, preferred_element_type=jnp.float32)
    dscore = (prob * (dprob - delta[:, None])).astype(jnp.bfloat16)
    d_query = jnp.dot(dscore, all_keys, preferred_element_type=jnp.float32) * scale

    stats = jnp.take(xor_gather(jnp.stack([lse, delta], axis=0), ("zh", "y", "core")), owner, axis=0)
    all_lse = stats[:, 0].reshape(total_rows)
    all_delta = stats[:, 1].reshape(total_rows)

    k_open = jnp.dot(jnp.dot(all_block, mask_f, precision=HI), own_block.T, precision=HI) > 0.5
    k_allowed = (own_pos[None, :] <= pos[:, None]) & (
        k_open | (own_pos[None, :] // BLK == pos[:, None] // BLK)
    )
    k_bias = jnp.dot(all_onehot, jnp.dot(table, role_onehot.T, precision=HI), precision=HI)
    score_t = jnp.dot(all_queries, own_keys.T, preferred_element_type=jnp.float32) * scale + k_bias
    prob_t = jnp.where(k_allowed, jnp.exp(score_t - all_lse[:, None]), jnp.float32(0.0))
    dprob_t = jnp.dot(all_grads, own_values.T, preferred_element_type=jnp.float32)
    dscore_t = (prob_t * (dprob_t - all_delta[:, None])).astype(jnp.bfloat16)
    d_key = jnp.dot(dscore_t.T, all_queries, preferred_element_type=jnp.float32) * scale
    d_value = jnp.dot(prob_t.astype(jnp.bfloat16).T, all_grads, preferred_element_type=jnp.float32)

    partial = shifted_all(jnp.stack([d_key, d_value], axis=0), "x")
    kv_sum = partial[0]
    for k in range(1, partial.shape[0]):
        kv_sum = kv_sum + partial[k]
    kv_all = shifted_all(kv_sum.astype(jnp.bfloat16), "g")
    kv_all = kv_all.transpose(1, 2, 0, 3).reshape(2, rows, -1)
    return (out, d_query.astype(jnp.bfloat16), kv_all[0], kv_all[1])


def solution(mesh):
    ctx_size = mesh.shape["ctx"]
    tp_size = mesh.shape["tp"]
    devices = np.asarray(mesh.devices).reshape(ctx_size, tp_size // GROUP, GROUP)
    inner = Mesh(devices.reshape(2, ctx_size // 4, 2, tp_size // GROUP, GROUP), ("zh", "y", "core", "g", "x"))
    heads = ("g", "x")
    seq = ("zh", "y", "core")
    return jax.shard_map(
        on_device,
        mesh=inner,
        in_specs=(
            P(seq, heads),
            P(seq, None),
            P(seq, None),
            P(seq),
            P(heads, None, None),
            P(),
            P(seq, heads),
        ),
        out_specs=(P(seq, heads), P(seq, heads), P(seq, None), P(seq, None)),
        check_vma=False,
    )
```

```python
import math

import jax
import jax.numpy as jnp
import numpy as np
from jax import lax
from jax.sharding import Mesh
from jax.sharding import PartitionSpec as P

HS = 128
GROUP = 4
BLK = 128
NEG = -1e30
HI = lax.Precision.HIGHEST


def xor_pairs(count, bit):
    return [(i, i ^ bit) for i in range(count)]


def xor_gather(block, axis):
    count = lax.axis_size(axis)
    me = lax.axis_index(axis)
    held = block[None]
    bit = 1
    while bit < count:
        held = jnp.concatenate([held, lax.ppermute(held, axis, xor_pairs(count, bit))], axis=0)
        bit *= 2
    return jnp.take(held, me ^ jnp.arange(count), axis=0)


def xor_sum(value, axis):
    count = lax.axis_size(axis)
    bit = 1
    while bit < count:
        value = value + lax.ppermute(value, axis, xor_pairs(count, bit))
        bit *= 2
    return value


def bruck_gather(block, axis):
    count = lax.axis_size(axis)
    me = lax.axis_index(axis)
    held = block[None]
    step = 1
    while step < count:
        part = held[: min(step, count - step)]
        pairs = [(i, (i - step) % count) for i in range(count)]
        held = jnp.concatenate([held, lax.ppermute(part, axis, pairs)], axis=0)
        step *= 2
    return jnp.take(held, (jnp.arange(count) - me) % count, axis=0)


def shift_pairs(count, step):
    return [(i, (i + step) % count) for i in range(count)]


def gather_ctx(full, half):
    zh = lax.axis_index("zh")
    y = lax.axis_index("y")
    core = lax.axis_index("core")
    ny = lax.axis_size("y")
    ncore = lax.axis_size("core")
    nz = lax.axis_size("zh")

    def index_of(z, yy, cc):
        return (z * ny + yy) * ncore + cc

    chip = jnp.concatenate([full, lax.ppermute(half, "zh", xor_pairs(nz, 1))], axis=0)[None]
    blocks = [chip]
    owners = [jnp.stack([index_of(zh, y, core), index_of(1 - zh, y, core)])]
    left = chip
    right = chip
    swapped = []
    for step in range(1, ny // 2 + 1):
        if step == ny // 4 + 1:
            swapped.append(lax.ppermute(jnp.concatenate(blocks, axis=0), "core", xor_pairs(ncore, 1)))
            sent = len(blocks)
        left = lax.ppermute(left, "y", shift_pairs(ny, 1))
        blocks.append(left)
        yy = (y - step) % ny
        owners.append(jnp.stack([index_of(zh, yy, core), index_of(1 - zh, yy, core)]))
        if step < ny - step:
            right = lax.ppermute(right, "y", shift_pairs(ny, -1))
            blocks.append(right)
            yy = (y + step) % ny
            owners.append(jnp.stack([index_of(zh, yy, core), index_of(1 - zh, yy, core)]))
    mine = jnp.concatenate(blocks, axis=0)
    owner = jnp.stack(owners)
    swapped.append(lax.ppermute(jnp.concatenate(blocks[sent:], axis=0), "core", xor_pairs(ncore, 1)))
    every = jnp.concatenate([mine] + swapped, axis=0)
    owner = jnp.concatenate([owner, owner - core + (1 - core)], axis=0)
    rows = full.shape[0]
    return every[:, :rows], every[:, rows:], owner[:, 0], owner[:, 1]


def shifted_all(value, axis):
    count = lax.axis_size(axis)
    me = lax.axis_index(axis)
    parts = [value] + [lax.ppermute(value, axis, shift_pairs(count, s)) for s in range(1, count)]
    return jnp.take(jnp.stack(parts), (me - jnp.arange(count)) % count, axis=0)


def on_device(queries, keys, values, roles, role_table, block_mask, d_out):
    rows = queries.shape[0]
    role_count = role_table.shape[1]
    scale = 1.0 / math.sqrt(HS)
    ctx_index = (lax.axis_index("zh") * lax.axis_size("y") + lax.axis_index("y")) * lax.axis_size(
        "core"
    ) + lax.axis_index("core")
    group = lax.axis_index("g")
    own_keys = lax.dynamic_slice_in_dim(keys, group * HS, HS, 1)
    own_values = lax.dynamic_slice_in_dim(values, group * HS, HS, 1)
    table = role_table[0]

    role_onehot = (roles[:, None] == jnp.arange(role_count)[None, :]).astype(jnp.float32)
    role_rows = jnp.zeros((16, rows), jnp.bfloat16).at[0].set(roles.astype(jnp.bfloat16))
    packed = jnp.concatenate([own_keys, own_values, queries, d_out, role_rows], axis=0)
    early = lax.axis_index("zh") == 0
    half = jnp.concatenate(
        [jnp.where(early, own_keys, queries), jnp.where(early, own_values, d_out), role_rows], axis=0
    )
    near, far, near_owner, far_owner = gather_ctx(packed, half)
    owner = jnp.concatenate([near_owner, far_owner])
    total_rows = 2 * near.shape[0] * rows

    def joined(near_part, far_part):
        return jnp.concatenate([near_part, far_part], axis=0).reshape((total_rows,) + near_part.shape[2:])

    all_keys = joined(near[:, 0:rows], far[:, 0:rows])
    all_values = joined(near[:, rows : 2 * rows], far[:, rows : 2 * rows])
    all_queries = joined(near[:, 2 * rows : 3 * rows], far[:, 0:rows])
    all_grads = joined(near[:, 3 * rows : 4 * rows], far[:, rows : 2 * rows])
    all_roles = joined(near[:, 4 * rows], far[:, 2 * rows]).astype(jnp.int32)
    all_onehot = (all_roles[:, None] == jnp.arange(role_count)[None, :]).astype(jnp.float32)

    pos = (owner[:, None] * rows + jnp.arange(rows)[None, :]).reshape(total_rows)
    own_pos = ctx_index * rows + jnp.arange(rows)
    mask_f = block_mask.astype(jnp.float32)
    all_block = (pos[:, None] // BLK == jnp.arange(block_mask.shape[0])[None, :]).astype(jnp.float32)
    own_block = (own_pos[:, None] // BLK == jnp.arange(block_mask.shape[0])[None, :]).astype(jnp.float32)

    q_open = jnp.dot(jnp.dot(own_block, mask_f, precision=HI), all_block.T, precision=HI) > 0.5
    q_allowed = (pos[None, :] <= own_pos[:, None]) & (
        q_open | (pos[None, :] // BLK == own_pos[:, None] // BLK)
    )
    q_bias = jnp.dot(jnp.dot(role_onehot, table, precision=HI), all_onehot.T, precision=HI)
    score = jnp.dot(queries, all_keys.T, preferred_element_type=jnp.float32) * scale + q_bias
    score = jnp.where(q_allowed, score, jnp.float32(NEG))
    top = jnp.max(score, axis=-1)
    expo = jnp.where(q_allowed, jnp.exp(score - top[:, None]), jnp.float32(0.0))
    total = jnp.sum(expo, axis=-1)
    out = jnp.dot(expo.astype(jnp.bfloat16), all_values, preferred_element_type=jnp.float32)
    out = (out / total[:, None]).astype(jnp.bfloat16)
    lse = top + jnp.log(total)
    delta = jnp.sum(d_out.astype(jnp.float32) * out.astype(jnp.float32), axis=-1)
    prob = jnp.where(q_allowed, jnp.exp(score - lse[:, None]), jnp.float32(0.0))
    dprob = jnp.dot(d_out, all_values.T, preferred_element_type=jnp.float32)
    dscore = (prob * (dprob - delta[:, None])).astype(jnp.bfloat16)
    d_query = jnp.dot(dscore, all_keys, preferred_element_type=jnp.float32) * scale

    stats = jnp.take(xor_gather(jnp.stack([lse, delta], axis=0), ("zh", "y", "core")), owner, axis=0)
    all_lse = stats[:, 0].reshape(total_rows)
    all_delta = stats[:, 1].reshape(total_rows)

    k_open = jnp.dot(jnp.dot(all_block, mask_f, precision=HI), own_block.T, precision=HI) > 0.5
    k_allowed = (own_pos[None, :] <= pos[:, None]) & (
        k_open | (own_pos[None, :] // BLK == pos[:, None] // BLK)
    )
    k_bias = jnp.dot(all_onehot, jnp.dot(table, role_onehot.T, precision=HI), precision=HI)
    score_t = jnp.dot(all_queries, own_keys.T, preferred_element_type=jnp.float32) * scale + k_bias
    prob_t = jnp.where(k_allowed, jnp.exp(score_t - all_lse[:, None]), jnp.float32(0.0))
    dprob_t = jnp.dot(all_grads, own_values.T, preferred_element_type=jnp.float32)
    dscore_t = (prob_t * (dprob_t - all_delta[:, None])).astype(jnp.bfloat16)
    d_key = jnp.dot(dscore_t.T, all_queries, preferred_element_type=jnp.float32) * scale
    d_value = jnp.dot(prob_t.astype(jnp.bfloat16).T, all_grads, preferred_element_type=jnp.float32)

    partial = shifted_all(jnp.stack([d_key, d_value], axis=0), "x")
    kv_sum = partial[0]
    for k in range(1, partial.shape[0]):
        kv_sum = kv_sum + partial[k]
    kv_all = shifted_all(kv_sum.astype(jnp.bfloat16), "g")
    kv_all = kv_all.transpose(1, 2, 0, 3).reshape(2, rows, -1)
    return (out, d_query.astype(jnp.bfloat16), kv_all[0], kv_all[1])


def solution(mesh):
    ctx_size = mesh.shape["ctx"]
    tp_size = mesh.shape["tp"]
    devices = np.asarray(mesh.devices).reshape(ctx_size, tp_size // GROUP, GROUP)
    inner = Mesh(devices.reshape(2, ctx_size // 4, 2, tp_size // GROUP, GROUP), ("zh", "y", "core", "g", "x"))
    heads = ("g", "x")
    seq = ("zh", "y", "core")
    return jax.shard_map(
        on_device,
        mesh=inner,
        in_specs=(
            P(seq, heads),
            P(seq, None),
            P(seq, None),
            P(seq),
            P(heads, None, None),
            P(),
            P(seq, heads),
        ),
        out_specs=(P(seq, heads), P(seq, heads), P(seq, None), P(seq, None)),
        check_vma=False,
    )
```

```python
import math

import jax
import jax.numpy as jnp
import numpy as np
from jax import lax
from jax.sharding import Mesh
from jax.sharding import PartitionSpec as P

HS = 128
GROUP = 4
BLK = 128
NEG = -1e30
HI = lax.Precision.HIGHEST


def xor_pairs(count, bit):
    return [(i, i ^ bit) for i in range(count)]


def xor_gather(block, axis):
    count = lax.axis_size(axis)
    me = lax.axis_index(axis)
    held = block[None]
    bit = 1
    while bit < count:
        held = jnp.concatenate([held, lax.ppermute(held, axis, xor_pairs(count, bit))], axis=0)
        bit *= 2
    return jnp.take(held, me ^ jnp.arange(count), axis=0)


def xor_sum(value, axis):
    count = lax.axis_size(axis)
    bit = 1
    while bit < count:
        value = value + lax.ppermute(value, axis, xor_pairs(count, bit))
        bit *= 2
    return value


def bruck_gather(block, axis):
    count = lax.axis_size(axis)
    me = lax.axis_index(axis)
    held = block[None]
    step = 1
    while step < count:
        part = held[: min(step, count - step)]
        pairs = [(i, (i - step) % count) for i in range(count)]
        held = jnp.concatenate([held, lax.ppermute(part, axis, pairs)], axis=0)
        step *= 2
    return jnp.take(held, (jnp.arange(count) - me) % count, axis=0)


def shift_pairs(count, step):
    return [(i, (i + step) % count) for i in range(count)]


def gather_ctx(full, half, slot):
    zh = lax.axis_index("zh")
    y = lax.axis_index("y")
    core = lax.axis_index("core")
    ny = lax.axis_size("y")
    ncore = lax.axis_size("core")
    nz = lax.axis_size("zh")

    def index_of(z, yy, cc):
        return (z * ny + yy) * ncore + cc

    chip = jnp.concatenate([full, lax.ppermute(half, "zh", xor_pairs(nz, 1))], axis=0)[None]
    blocks = [chip]
    owners = [jnp.stack([index_of(zh, y, core), index_of(1 - zh, y, core)])]
    left = chip
    right = chip
    for step in range(1, ny // 2 + 1):
        left = lax.ppermute(left, "y", shift_pairs(ny, 1))
        blocks.append(left)
        yy = (y - step) % ny
        owners.append(jnp.stack([index_of(zh, yy, core), index_of(1 - zh, yy, core)]))
        if step < ny - step:
            right = lax.ppermute(right, "y", shift_pairs(ny, -1))
            blocks.append(right)
            yy = (y + step) % ny
            owners.append(jnp.stack([index_of(zh, yy, core), index_of(1 - zh, yy, core)]))
    mine = jnp.concatenate(blocks, axis=0)
    owner = jnp.stack(owners)
    rows = full.shape[0]
    pair = 2 * slot
    near = mine[:, :rows]
    earlier = owner[:, 0] < index_of(zh, y, 1 - core)
    near_half = jnp.concatenate(
        [jnp.where(earlier[:, None, None], near[:, :pair], near[:, pair : 2 * pair]), near[:, 2 * pair :]],
        axis=1,
    )
    other = lax.ppermute(jnp.concatenate([near_half, mine[:, rows:]], axis=1), "core", xor_pairs(ncore, 1))
    other_owner = owner - core + (1 - core)
    size = half.shape[0]
    halves = jnp.concatenate([mine[:, rows:], other[:, :size], other[:, size:]], axis=0)
    half_owner = jnp.concatenate([owner[:, 1], other_owner[:, 0], other_owner[:, 1]])
    return near, halves, owner[:, 0], half_owner


def shifted_all(value, axis):
    count = lax.axis_size(axis)
    me = lax.axis_index(axis)
    parts = [value] + [lax.ppermute(value, axis, shift_pairs(count, s)) for s in range(1, count)]
    return jnp.take(jnp.stack(parts), (me - jnp.arange(count)) % count, axis=0)


def on_device(queries, keys, values, roles, role_table, block_mask, d_out):
    rows = queries.shape[0]
    role_count = role_table.shape[1]
    scale = 1.0 / math.sqrt(HS)
    ctx_index = (lax.axis_index("zh") * lax.axis_size("y") + lax.axis_index("y")) * lax.axis_size(
        "core"
    ) + lax.axis_index("core")
    group = lax.axis_index("g")
    own_keys = lax.dynamic_slice_in_dim(keys, group * HS, HS, 1)
    own_values = lax.dynamic_slice_in_dim(values, group * HS, HS, 1)
    table = role_table[0]

    role_onehot = (roles[:, None] == jnp.arange(role_count)[None, :]).astype(jnp.float32)
    role_rows = jnp.zeros((16, rows), jnp.bfloat16).at[0].set(roles.astype(jnp.bfloat16))
    packed = jnp.concatenate([own_keys, own_values, queries, d_out, role_rows], axis=0)
    early = lax.axis_index("zh") == 0
    half = jnp.concatenate(
        [jnp.where(early, own_keys, queries), jnp.where(early, own_values, d_out), role_rows], axis=0
    )
    near, far, near_owner, far_owner = gather_ctx(packed, half, rows)
    owner = jnp.concatenate([near_owner, far_owner])
    total_rows = (near.shape[0] + far.shape[0]) * rows

    def joined(near_part, far_part):
        return jnp.concatenate([near_part, far_part], axis=0).reshape((total_rows,) + near_part.shape[2:])

    all_keys = joined(near[:, 0:rows], far[:, 0:rows])
    all_values = joined(near[:, rows : 2 * rows], far[:, rows : 2 * rows])
    all_queries = joined(near[:, 2 * rows : 3 * rows], far[:, 0:rows])
    all_grads = joined(near[:, 3 * rows : 4 * rows], far[:, rows : 2 * rows])
    all_roles = joined(near[:, 4 * rows], far[:, 2 * rows]).astype(jnp.int32)
    all_onehot = (all_roles[:, None] == jnp.arange(role_count)[None, :]).astype(jnp.float32)

    pos = (owner[:, None] * rows + jnp.arange(rows)[None, :]).reshape(total_rows)
    own_pos = ctx_index * rows + jnp.arange(rows)
    mask_f = block_mask.astype(jnp.float32)
    all_block = (pos[:, None] // BLK == jnp.arange(block_mask.shape[0])[None, :]).astype(jnp.float32)
    own_block = (own_pos[:, None] // BLK == jnp.arange(block_mask.shape[0])[None, :]).astype(jnp.float32)

    q_open = jnp.dot(jnp.dot(own_block, mask_f, precision=HI), all_block.T, precision=HI) > 0.5
    q_allowed = (pos[None, :] <= own_pos[:, None]) & (
        q_open | (pos[None, :] // BLK == own_pos[:, None] // BLK)
    )
    q_bias = jnp.dot(jnp.dot(role_onehot, table, precision=HI), all_onehot.T, precision=HI)
    score = jnp.dot(queries, all_keys.T, preferred_element_type=jnp.float32) * scale + q_bias
    score = jnp.where(q_allowed, score, jnp.float32(NEG))
    top = jnp.max(score, axis=-1)
    expo = jnp.where(q_allowed, jnp.exp(score - top[:, None]), jnp.float32(0.0))
    total = jnp.sum(expo, axis=-1)
    out = jnp.dot(expo.astype(jnp.bfloat16), all_values, preferred_element_type=jnp.float32)
    out = (out / total[:, None]).astype(jnp.bfloat16)
    lse = top + jnp.log(total)
    delta = jnp.sum(d_out.astype(jnp.float32) * out.astype(jnp.float32), axis=-1)
    prob = jnp.where(q_allowed, jnp.exp(score - lse[:, None]), jnp.float32(0.0))
    dprob = jnp.dot(d_out, all_values.T, preferred_element_type=jnp.float32)
    dscore = (prob * (dprob - delta[:, None])).astype(jnp.bfloat16)
    d_query = jnp.dot(dscore, all_keys, preferred_element_type=jnp.float32) * scale

    stats = jnp.take(xor_gather(jnp.stack([lse, delta], axis=0), ("zh", "y", "core")), owner, axis=0)
    all_lse = stats[:, 0].reshape(total_rows)
    all_delta = stats[:, 1].reshape(total_rows)

    k_open = jnp.dot(jnp.dot(all_block, mask_f, precision=HI), own_block.T, precision=HI) > 0.5
    k_allowed = (own_pos[None, :] <= pos[:, None]) & (
        k_open | (own_pos[None, :] // BLK == pos[:, None] // BLK)
    )
    k_bias = jnp.dot(all_onehot, jnp.dot(table, role_onehot.T, precision=HI), precision=HI)
    score_t = jnp.dot(all_queries, own_keys.T, preferred_element_type=jnp.float32) * scale + k_bias
    prob_t = jnp.where(k_allowed, jnp.exp(score_t - all_lse[:, None]), jnp.float32(0.0))
    dprob_t = jnp.dot(all_grads, own_values.T, preferred_element_type=jnp.float32)
    dscore_t = (prob_t * (dprob_t - all_delta[:, None])).astype(jnp.bfloat16)
    d_key = jnp.dot(dscore_t.T, all_queries, preferred_element_type=jnp.float32) * scale
    d_value = jnp.dot(prob_t.astype(jnp.bfloat16).T, all_grads, preferred_element_type=jnp.float32)

    partial = shifted_all(jnp.stack([d_key, d_value], axis=0), "x")
    kv_sum = partial[0]
    for k in range(1, partial.shape[0]):
        kv_sum = kv_sum + partial[k]
    kv_all = shifted_all(kv_sum.astype(jnp.bfloat16), "g")
    kv_all = kv_all.transpose(1, 2, 0, 3).reshape(2, rows, -1)
    return (out, d_query.astype(jnp.bfloat16), kv_all[0], kv_all[1])


def solution(mesh):
    ctx_size = mesh.shape["ctx"]
    tp_size = mesh.shape["tp"]
    devices = np.asarray(mesh.devices).reshape(ctx_size, tp_size // GROUP, GROUP)
    inner = Mesh(devices.reshape(2, ctx_size // 4, 2, tp_size // GROUP, GROUP), ("zh", "y", "core", "g", "x"))
    heads = ("g", "x")
    seq = ("zh", "y", "core")
    return jax.shard_map(
        on_device,
        mesh=inner,
        in_specs=(
            P(seq, heads),
            P(seq, None),
            P(seq, None),
            P(seq),
            P(heads, None, None),
            P(),
            P(seq, heads),
        ),
        out_specs=(P(seq, heads), P(seq, heads), P(seq, None), P(seq, None)),
        check_vma=False,
    )
```

```python
import math

import jax
import jax.numpy as jnp
import numpy as np
from jax import lax
from jax.sharding import Mesh
from jax.sharding import PartitionSpec as P

HS = 128
GROUP = 4
BLK = 128
NEG = -1e30
HI = lax.Precision.HIGHEST


def xor_pairs(count, bit):
    return [(i, i ^ bit) for i in range(count)]


def xor_gather(block, axis):
    count = lax.axis_size(axis)
    me = lax.axis_index(axis)
    held = block[None]
    bit = 1
    while bit < count:
        held = jnp.concatenate([held, lax.ppermute(held, axis, xor_pairs(count, bit))], axis=0)
        bit *= 2
    return jnp.take(held, me ^ jnp.arange(count), axis=0)


def xor_sum(value, axis):
    count = lax.axis_size(axis)
    bit = 1
    while bit < count:
        value = value + lax.ppermute(value, axis, xor_pairs(count, bit))
        bit *= 2
    return value


def bruck_gather(block, axis):
    count = lax.axis_size(axis)
    me = lax.axis_index(axis)
    held = block[None]
    step = 1
    while step < count:
        part = held[: min(step, count - step)]
        pairs = [(i, (i - step) % count) for i in range(count)]
        held = jnp.concatenate([held, lax.ppermute(part, axis, pairs)], axis=0)
        step *= 2
    return jnp.take(held, (jnp.arange(count) - me) % count, axis=0)


def shift_pairs(count, step):
    return [(i, (i + step) % count) for i in range(count)]


def gather_ctx(full, half, slot):
    zh = lax.axis_index("zh")
    y = lax.axis_index("y")
    core = lax.axis_index("core")
    ny = lax.axis_size("y")
    ncore = lax.axis_size("core")
    nz = lax.axis_size("zh")

    def index_of(z, yy, cc):
        return (z * ny + yy) * ncore + cc

    chip = jnp.concatenate([full, lax.ppermute(half, "zh", xor_pairs(nz, 1))], axis=0)[None]
    blocks = [chip]
    owners = [jnp.stack([index_of(zh, y, core), index_of(1 - zh, y, core)])]
    left = chip
    right = chip
    for step in range(1, ny // 2 + 1):
        left = lax.ppermute(left, "y", shift_pairs(ny, 1))
        blocks.append(left)
        yy = (y - step) % ny
        owners.append(jnp.stack([index_of(zh, yy, core), index_of(1 - zh, yy, core)]))
        if step < ny - step:
            right = lax.ppermute(right, "y", shift_pairs(ny, -1))
            blocks.append(right)
            yy = (y + step) % ny
            owners.append(jnp.stack([index_of(zh, yy, core), index_of(1 - zh, yy, core)]))
    mine = jnp.concatenate(blocks, axis=0)
    owner = jnp.stack(owners)
    rows = full.shape[0]
    pair = 2 * slot
    near = mine[:, :rows]
    earlier = owner[:, 0] < index_of(zh, y, 1 - core)
    near_half = jnp.concatenate(
        [jnp.where(earlier[:, None, None], near[:, :pair], near[:, pair : 2 * pair]), near[:, 2 * pair :]],
        axis=1,
    )
    other = lax.ppermute(jnp.concatenate([near_half, mine[:, rows:]], axis=1), "core", xor_pairs(ncore, 1))
    other_owner = owner - core + (1 - core)
    size = half.shape[0]
    halves = jnp.concatenate([mine[:, rows:], other[:, :size], other[:, size:]], axis=0)
    half_owner = jnp.concatenate([owner[:, 1], other_owner[:, 0], other_owner[:, 1]])
    return near, halves, owner[:, 0], half_owner


def shifted_all(value, axis):
    count = lax.axis_size(axis)
    me = lax.axis_index(axis)
    parts = [value] + [lax.ppermute(value, axis, shift_pairs(count, s)) for s in range(1, count)]
    return jnp.take(jnp.stack(parts), (me - jnp.arange(count)) % count, axis=0)


def on_device(queries, keys, values, roles, role_table, block_mask, d_out):
    rows = queries.shape[0]
    role_count = role_table.shape[1]
    scale = 1.0 / math.sqrt(HS)
    ctx_index = (lax.axis_index("zh") * lax.axis_size("y") + lax.axis_index("y")) * lax.axis_size(
        "core"
    ) + lax.axis_index("core")
    group = lax.axis_index("g")
    own_keys = lax.dynamic_slice_in_dim(keys, group * HS, HS, 1)
    own_values = lax.dynamic_slice_in_dim(values, group * HS, HS, 1)
    table = role_table[0]

    role_rows = jnp.zeros((16, rows), jnp.bfloat16).at[0].set(roles.astype(jnp.bfloat16))
    packed = jnp.concatenate([own_keys, own_values, queries, d_out, role_rows], axis=0)
    early = lax.axis_index("zh") == 0
    half = jnp.concatenate(
        [jnp.where(early, own_keys, queries), jnp.where(early, own_values, d_out), role_rows], axis=0
    )
    near, far, near_owner, far_owner = gather_ctx(packed, half, rows)
    owner = jnp.concatenate([near_owner, far_owner])
    total_rows = (near.shape[0] + far.shape[0]) * rows

    def joined(near_part, far_part):
        return jnp.concatenate([near_part, far_part], axis=0).reshape((total_rows,) + near_part.shape[2:])

    all_keys = joined(near[:, 0:rows], far[:, 0:rows])
    all_values = joined(near[:, rows : 2 * rows], far[:, rows : 2 * rows])
    all_queries = joined(near[:, 2 * rows : 3 * rows], far[:, 0:rows])
    all_grads = joined(near[:, 3 * rows : 4 * rows], far[:, rows : 2 * rows])
    all_roles = joined(near[:, 4 * rows], far[:, 2 * rows]).astype(jnp.int32)
    all_onehot = (all_roles[:, None] == jnp.arange(role_count)[None, :]).astype(jnp.float32)

    pos = (owner[:, None] * rows + jnp.arange(rows)[None, :]).reshape(total_rows)
    own_pos = ctx_index * rows + jnp.arange(rows)
    mask_f = block_mask.astype(jnp.float32)
    all_block = (pos[:, None] // BLK == jnp.arange(block_mask.shape[0])[None, :]).astype(jnp.float32)
    own_block = (own_pos[:, None] // BLK == jnp.arange(block_mask.shape[0])[None, :]).astype(jnp.float32)

    own_rows = jnp.take(mask_f, own_pos // BLK, axis=0).astype(jnp.bfloat16)
    q_open = jnp.dot(own_rows, all_block.T.astype(jnp.bfloat16), preferred_element_type=jnp.float32) > 0.5
    q_allowed = (pos[None, :] <= own_pos[:, None]) & (
        q_open | (pos[None, :] // BLK == own_pos[:, None] // BLK)
    )
    q_bias = jnp.dot(jnp.take(table, roles, axis=0), all_onehot.T, precision=HI)
    score = jnp.dot(queries, all_keys.T, preferred_element_type=jnp.float32) * scale + q_bias
    score = jnp.where(q_allowed, score, jnp.float32(NEG))
    top = jnp.max(score, axis=-1)
    expo = jnp.where(q_allowed, jnp.exp(score - top[:, None]), jnp.float32(0.0))
    total = jnp.sum(expo, axis=-1)
    out = jnp.dot(expo.astype(jnp.bfloat16), all_values, preferred_element_type=jnp.float32)
    out = (out / total[:, None]).astype(jnp.bfloat16)
    lse = top + jnp.log(total)
    delta = jnp.sum(d_out.astype(jnp.float32) * out.astype(jnp.float32), axis=-1)
    prob = jnp.where(q_allowed, jnp.exp(score - lse[:, None]), jnp.float32(0.0))
    dprob = jnp.dot(d_out, all_values.T, preferred_element_type=jnp.float32)
    dscore = (prob * (dprob - delta[:, None])).astype(jnp.bfloat16)
    d_query = jnp.dot(dscore, all_keys, preferred_element_type=jnp.float32) * scale

    stats = jnp.take(xor_gather(jnp.stack([lse, delta], axis=0), ("zh", "y", "core")), owner, axis=0)
    all_lse = stats[:, 0].reshape(total_rows)
    all_delta = stats[:, 1].reshape(total_rows)

    all_rows = jnp.take(mask_f, pos // BLK, axis=0).astype(jnp.bfloat16)
    k_open = jnp.dot(all_rows, own_block.T.astype(jnp.bfloat16), preferred_element_type=jnp.float32) > 0.5
    k_allowed = (own_pos[None, :] <= pos[:, None]) & (
        k_open | (own_pos[None, :] // BLK == pos[:, None] // BLK)
    )
    k_bias = jnp.dot(all_onehot, jnp.take(table, roles, axis=1), precision=HI)
    score_t = jnp.dot(all_queries, own_keys.T, preferred_element_type=jnp.float32) * scale + k_bias
    prob_t = jnp.where(k_allowed, jnp.exp(score_t - all_lse[:, None]), jnp.float32(0.0))
    dprob_t = jnp.dot(all_grads, own_values.T, preferred_element_type=jnp.float32)
    dscore_t = (prob_t * (dprob_t - all_delta[:, None])).astype(jnp.bfloat16)
    d_key = jnp.dot(dscore_t.T, all_queries, preferred_element_type=jnp.float32) * scale
    d_value = jnp.dot(prob_t.astype(jnp.bfloat16).T, all_grads, preferred_element_type=jnp.float32)

    partial = shifted_all(jnp.stack([d_key, d_value], axis=0), "x")
    kv_sum = partial[0]
    for k in range(1, partial.shape[0]):
        kv_sum = kv_sum + partial[k]
    kv_all = shifted_all(kv_sum.astype(jnp.bfloat16), "g")
    kv_all = kv_all.transpose(1, 2, 0, 3).reshape(2, rows, -1)
    return (out, d_query.astype(jnp.bfloat16), kv_all[0], kv_all[1])


def solution(mesh):
    ctx_size = mesh.shape["ctx"]
    tp_size = mesh.shape["tp"]
    devices = np.asarray(mesh.devices).reshape(ctx_size, tp_size // GROUP, GROUP)
    inner = Mesh(devices.reshape(2, ctx_size // 4, 2, tp_size // GROUP, GROUP), ("zh", "y", "core", "g", "x"))
    heads = ("g", "x")
    seq = ("zh", "y", "core")
    return jax.shard_map(
        on_device,
        mesh=inner,
        in_specs=(
            P(seq, heads),
            P(seq, None),
            P(seq, None),
            P(seq),
            P(heads, None, None),
            P(),
            P(seq, heads),
        ),
        out_specs=(P(seq, heads), P(seq, heads), P(seq, None), P(seq, None)),
        check_vma=False,
    )
```

```python
import math

import jax
import jax.numpy as jnp
import numpy as np
from jax import lax
from jax.sharding import Mesh
from jax.sharding import PartitionSpec as P

HS = 128
GROUP = 4
BLK = 128
NEG = -1e30
HI = lax.Precision.HIGHEST


def xor_pairs(count, bit):
    return [(i, i ^ bit) for i in range(count)]


def xor_gather(block, axis):
    count = lax.axis_size(axis)
    me = lax.axis_index(axis)
    held = block[None]
    bit = 1
    while bit < count:
        held = jnp.concatenate([held, lax.ppermute(held, axis, xor_pairs(count, bit))], axis=0)
        bit *= 2
    return jnp.take(held, me ^ jnp.arange(count), axis=0)


def xor_sum(value, axis):
    count = lax.axis_size(axis)
    bit = 1
    while bit < count:
        value = value + lax.ppermute(value, axis, xor_pairs(count, bit))
        bit *= 2
    return value


def bruck_gather(block, axis):
    count = lax.axis_size(axis)
    me = lax.axis_index(axis)
    held = block[None]
    step = 1
    while step < count:
        part = held[: min(step, count - step)]
        pairs = [(i, (i - step) % count) for i in range(count)]
        held = jnp.concatenate([held, lax.ppermute(part, axis, pairs)], axis=0)
        step *= 2
    return jnp.take(held, (jnp.arange(count) - me) % count, axis=0)


def shift_pairs(count, step):
    return [(i, (i + step) % count) for i in range(count)]


def gather_ctx(full, half, slot):
    zh = lax.axis_index("zh")
    y = lax.axis_index("y")
    core = lax.axis_index("core")
    ny = lax.axis_size("y")
    ncore = lax.axis_size("core")
    nz = lax.axis_size("zh")

    def index_of(z, yy, cc):
        return (z * ny + yy) * ncore + cc

    chip = jnp.concatenate([full, lax.ppermute(half, "zh", xor_pairs(nz, 1))], axis=0)[None]
    blocks = [chip]
    owners = [jnp.stack([index_of(zh, y, core), index_of(1 - zh, y, core)])]
    left = chip
    right = chip
    for step in range(1, ny // 2 + 1):
        left = lax.ppermute(left, "y", shift_pairs(ny, 1))
        blocks.append(left)
        yy = (y - step) % ny
        owners.append(jnp.stack([index_of(zh, yy, core), index_of(1 - zh, yy, core)]))
        if step < ny - step:
            right = lax.ppermute(right, "y", shift_pairs(ny, -1))
            blocks.append(right)
            yy = (y + step) % ny
            owners.append(jnp.stack([index_of(zh, yy, core), index_of(1 - zh, yy, core)]))
    mine = jnp.concatenate(blocks, axis=0)
    owner = jnp.stack(owners)
    rows = full.shape[0]
    pair = 2 * slot
    near = mine[:, :rows]
    earlier = owner[:, 0] < index_of(zh, y, 1 - core)
    near_half = jnp.concatenate(
        [jnp.where(earlier[:, None, None], near[:, :pair], near[:, pair : 2 * pair]), near[:, 2 * pair :]],
        axis=1,
    )
    other = lax.ppermute(jnp.concatenate([near_half, mine[:, rows:]], axis=1), "core", xor_pairs(ncore, 1))
    other_owner = owner - core + (1 - core)
    size = half.shape[0]
    halves = jnp.concatenate([mine[:, rows:], other[:, :size], other[:, size:]], axis=0)
    half_owner = jnp.concatenate([owner[:, 1], other_owner[:, 0], other_owner[:, 1]])
    return near, halves, owner[:, 0], half_owner


def shifted_all(value, axis):
    count = lax.axis_size(axis)
    me = lax.axis_index(axis)
    parts = [value] + [lax.ppermute(value, axis, shift_pairs(count, s)) for s in range(1, count)]
    return jnp.take(jnp.stack(parts), (me - jnp.arange(count)) % count, axis=0)


def on_device(queries, keys, values, roles, role_table, block_mask, d_out):
    rows = queries.shape[0]
    role_count = role_table.shape[1]
    scale = 1.0 / math.sqrt(HS)
    ctx_index = (lax.axis_index("zh") * lax.axis_size("y") + lax.axis_index("y")) * lax.axis_size(
        "core"
    ) + lax.axis_index("core")
    group = lax.axis_index("g")
    own_keys = lax.dynamic_slice_in_dim(keys, group * HS, HS, 1)
    own_values = lax.dynamic_slice_in_dim(values, group * HS, HS, 1)
    table = role_table[0]

    role_rows = jnp.zeros((16, rows), jnp.bfloat16).at[0].set(roles.astype(jnp.bfloat16))
    packed = jnp.concatenate([own_keys, own_values, queries, d_out, role_rows], axis=0)
    early = lax.axis_index("zh") == 0
    half = jnp.concatenate(
        [jnp.where(early, own_keys, queries), jnp.where(early, own_values, d_out), role_rows], axis=0
    )
    near, far, near_owner, far_owner = gather_ctx(packed, half, rows)
    owner = jnp.concatenate([near_owner, far_owner])
    total_rows = (near.shape[0] + far.shape[0]) * rows

    def joined(near_part, far_part):
        return jnp.concatenate([near_part, far_part], axis=0).reshape((total_rows,) + near_part.shape[2:])

    all_keys = joined(near[:, 0:rows], far[:, 0:rows])
    all_values = joined(near[:, rows : 2 * rows], far[:, rows : 2 * rows])
    all_queries = joined(near[:, 2 * rows : 3 * rows], far[:, 0:rows])
    all_grads = joined(near[:, 3 * rows : 4 * rows], far[:, rows : 2 * rows])
    all_roles = joined(near[:, 4 * rows], far[:, 2 * rows]).astype(jnp.int32)
    all_onehot = (all_roles[:, None] == jnp.arange(role_count)[None, :]).astype(jnp.float32)

    pos = (owner[:, None] * rows + jnp.arange(rows)[None, :]).reshape(total_rows)
    own_pos = ctx_index * rows + jnp.arange(rows)
    all_block = (pos[:, None] // BLK == jnp.arange(block_mask.shape[0])[None, :]).astype(jnp.float32)
    own_block = (own_pos[:, None] // BLK == jnp.arange(block_mask.shape[0])[None, :]).astype(jnp.float32)

    mask_b = block_mask.astype(jnp.bfloat16)
    own_rows = jnp.dot(own_block.astype(jnp.bfloat16), mask_b).astype(jnp.bfloat16)
    q_open = jnp.dot(own_rows, all_block.T.astype(jnp.bfloat16), preferred_element_type=jnp.float32) > 0.5
    q_allowed = (pos[None, :] <= own_pos[:, None]) & (
        q_open | (pos[None, :] // BLK == own_pos[:, None] // BLK)
    )
    q_bias = jnp.dot(jnp.take(table, roles, axis=0), all_onehot.T, precision=HI)
    score = jnp.dot(queries, all_keys.T, preferred_element_type=jnp.float32) * scale + q_bias
    score = jnp.where(q_allowed, score, jnp.float32(NEG))
    top = jnp.max(score, axis=-1)
    expo = jnp.where(q_allowed, jnp.exp(score - top[:, None]), jnp.float32(0.0))
    total = jnp.sum(expo, axis=-1)
    out = jnp.dot(expo.astype(jnp.bfloat16), all_values, preferred_element_type=jnp.float32)
    out = (out / total[:, None]).astype(jnp.bfloat16)
    lse = top + jnp.log(total)
    delta = jnp.sum(d_out.astype(jnp.float32) * out.astype(jnp.float32), axis=-1)
    prob = jnp.where(q_allowed, jnp.exp(score - lse[:, None]), jnp.float32(0.0))
    dprob = jnp.dot(d_out, all_values.T, preferred_element_type=jnp.float32)
    dscore = (prob * (dprob - delta[:, None])).astype(jnp.bfloat16)
    d_query = jnp.dot(dscore, all_keys, preferred_element_type=jnp.float32) * scale

    stats = jnp.take(xor_gather(jnp.stack([lse, delta], axis=0), ("zh", "y", "core")), owner, axis=0)
    all_lse = stats[:, 0].reshape(total_rows)
    all_delta = stats[:, 1].reshape(total_rows)

    all_rows = jnp.dot(all_block.astype(jnp.bfloat16), mask_b).astype(jnp.bfloat16)
    k_open = jnp.dot(all_rows, own_block.T.astype(jnp.bfloat16), preferred_element_type=jnp.float32) > 0.5
    k_allowed = (own_pos[None, :] <= pos[:, None]) & (
        k_open | (own_pos[None, :] // BLK == pos[:, None] // BLK)
    )
    k_bias = jnp.dot(all_onehot, jnp.take(table.T, roles, axis=0).T, precision=HI)
    score_t = jnp.dot(all_queries, own_keys.T, preferred_element_type=jnp.float32) * scale + k_bias
    prob_t = jnp.where(k_allowed, jnp.exp(score_t - all_lse[:, None]), jnp.float32(0.0))
    dprob_t = jnp.dot(all_grads, own_values.T, preferred_element_type=jnp.float32)
    dscore_t = (prob_t * (dprob_t - all_delta[:, None])).astype(jnp.bfloat16)
    d_key = jnp.dot(dscore_t.T, all_queries, preferred_element_type=jnp.float32) * scale
    d_value = jnp.dot(prob_t.astype(jnp.bfloat16).T, all_grads, preferred_element_type=jnp.float32)

    partial = shifted_all(jnp.stack([d_key, d_value], axis=0), "x")
    kv_sum = partial[0]
    for k in range(1, partial.shape[0]):
        kv_sum = kv_sum + partial[k]
    kv_all = shifted_all(kv_sum.astype(jnp.bfloat16), "g")
    kv_all = kv_all.transpose(1, 2, 0, 3).reshape(2, rows, -1)
    return (out, d_query.astype(jnp.bfloat16), kv_all[0], kv_all[1])


def solution(mesh):
    ctx_size = mesh.shape["ctx"]
    tp_size = mesh.shape["tp"]
    devices = np.asarray(mesh.devices).reshape(ctx_size, tp_size // GROUP, GROUP)
    inner = Mesh(devices.reshape(2, ctx_size // 4, 2, tp_size // GROUP, GROUP), ("zh", "y", "core", "g", "x"))
    heads = ("g", "x")
    seq = ("zh", "y", "core")
    return jax.shard_map(
        on_device,
        mesh=inner,
        in_specs=(
            P(seq, heads),
            P(seq, None),
            P(seq, None),
            P(seq),
            P(heads, None, None),
            P(),
            P(seq, heads),
        ),
        out_specs=(P(seq, heads), P(seq, heads), P(seq, None), P(seq, None)),
        check_vma=False,
    )
```

```python
import math

import jax
import jax.numpy as jnp
import numpy as np
from jax import lax
from jax.sharding import Mesh
from jax.sharding import PartitionSpec as P

HS = 128
GROUP = 4
BLK = 128
NEG = -1e30
HI = lax.Precision.HIGHEST


def xor_pairs(count, bit):
    return [(i, i ^ bit) for i in range(count)]


def xor_gather(block, axis):
    count = lax.axis_size(axis)
    me = lax.axis_index(axis)
    held = block[None]
    bit = 1
    while bit < count:
        held = jnp.concatenate([held, lax.ppermute(held, axis, xor_pairs(count, bit))], axis=0)
        bit *= 2
    return jnp.take(held, me ^ jnp.arange(count), axis=0)


def xor_sum(value, axis):
    count = lax.axis_size(axis)
    bit = 1
    while bit < count:
        value = value + lax.ppermute(value, axis, xor_pairs(count, bit))
        bit *= 2
    return value


def bruck_gather(block, axis):
    count = lax.axis_size(axis)
    me = lax.axis_index(axis)
    held = block[None]
    step = 1
    while step < count:
        part = held[: min(step, count - step)]
        pairs = [(i, (i - step) % count) for i in range(count)]
        held = jnp.concatenate([held, lax.ppermute(part, axis, pairs)], axis=0)
        step *= 2
    return jnp.take(held, (jnp.arange(count) - me) % count, axis=0)


def shift_pairs(count, step):
    return [(i, (i + step) % count) for i in range(count)]


def gather_ctx(full, half):
    zh = lax.axis_index("zh")
    y = lax.axis_index("y")
    core = lax.axis_index("core")
    ny = lax.axis_size("y")
    ncore = lax.axis_size("core")
    nz = lax.axis_size("zh")

    def index_of(z, yy, cc):
        return (z * ny + yy) * ncore + cc

    chip = jnp.concatenate([full, lax.ppermute(half, "zh", xor_pairs(nz, 1))], axis=0)[None]
    blocks = [chip]
    owners = [jnp.stack([index_of(zh, y, core), index_of(1 - zh, y, core)])]
    left = chip
    right = chip
    for step in range(1, ny // 2 + 1):
        left = lax.ppermute(left, "y", shift_pairs(ny, 1))
        blocks.append(left)
        yy = (y - step) % ny
        owners.append(jnp.stack([index_of(zh, yy, core), index_of(1 - zh, yy, core)]))
        if step < ny - step:
            right = lax.ppermute(right, "y", shift_pairs(ny, -1))
            blocks.append(right)
            yy = (y + step) % ny
            owners.append(jnp.stack([index_of(zh, yy, core), index_of(1 - zh, yy, core)]))
    mine = jnp.concatenate(blocks, axis=0)
    owner = jnp.stack(owners)
    other = lax.ppermute(mine, "core", xor_pairs(ncore, 1))
    every = jnp.concatenate([mine, other], axis=0)
    owner = jnp.concatenate([owner, owner - core + (1 - core)], axis=0)
    rows = full.shape[0]
    return every[:, :rows], every[:, rows:], owner[:, 0], owner[:, 1]


def shifted_all(value, axis):
    count = lax.axis_size(axis)
    me = lax.axis_index(axis)
    parts = [value] + [lax.ppermute(value, axis, shift_pairs(count, s)) for s in range(1, count)]
    return jnp.take(jnp.stack(parts), (me - jnp.arange(count)) % count, axis=0)


def on_device(queries, keys, values, roles, role_table, block_mask, d_out):
    rows = queries.shape[0]
    role_count = role_table.shape[1]
    scale = 1.0 / math.sqrt(HS)
    ctx_index = (lax.axis_index("zh") * lax.axis_size("y") + lax.axis_index("y")) * lax.axis_size(
        "core"
    ) + lax.axis_index("core")
    group = lax.axis_index("g")
    own_keys = lax.dynamic_slice_in_dim(keys, group * HS, HS, 1)
    own_values = lax.dynamic_slice_in_dim(values, group * HS, HS, 1)
    table = role_table[0]

    role_rows = jnp.zeros((16, rows), jnp.bfloat16).at[0].set(roles.astype(jnp.bfloat16))
    packed = jnp.concatenate([own_keys, own_values, queries, d_out, role_rows], axis=0)
    early = lax.axis_index("zh") == 0
    half = jnp.concatenate(
        [jnp.where(early, own_keys, queries), jnp.where(early, own_values, d_out), role_rows], axis=0
    )
    near, far, near_owner, far_owner = gather_ctx(packed, half)
    owner = jnp.concatenate([near_owner, far_owner])
    total_rows = 2 * near.shape[0] * rows

    def joined(near_part, far_part):
        return jnp.concatenate([near_part, far_part], axis=0).reshape((total_rows,) + near_part.shape[2:])

    all_keys = joined(near[:, 0:rows], far[:, 0:rows])
    all_values = joined(near[:, rows : 2 * rows], far[:, rows : 2 * rows])
    all_queries = joined(near[:, 2 * rows : 3 * rows], far[:, 0:rows])
    all_grads = joined(near[:, 3 * rows : 4 * rows], far[:, rows : 2 * rows])
    all_roles = joined(near[:, 4 * rows], far[:, 2 * rows]).astype(jnp.int32)
    all_onehot = (all_roles[:, None] == jnp.arange(role_count)[None, :]).astype(jnp.float32)

    pos = (owner[:, None] * rows + jnp.arange(rows)[None, :]).reshape(total_rows)
    own_pos = ctx_index * rows + jnp.arange(rows)
    all_block = (pos[:, None] // BLK == jnp.arange(block_mask.shape[0])[None, :]).astype(jnp.float32)
    own_block = (own_pos[:, None] // BLK == jnp.arange(block_mask.shape[0])[None, :]).astype(jnp.float32)

    mask_b = block_mask.astype(jnp.bfloat16)
    own_rows = jnp.dot(own_block.astype(jnp.bfloat16), mask_b).astype(jnp.bfloat16)
    q_open = jnp.dot(own_rows, all_block.T.astype(jnp.bfloat16), preferred_element_type=jnp.float32) > 0.5
    q_allowed = (pos[None, :] <= own_pos[:, None]) & (
        q_open | (pos[None, :] // BLK == own_pos[:, None] // BLK)
    )
    q_bias = jnp.dot(jnp.take(table, roles, axis=0), all_onehot.T, precision=HI)
    score = jnp.dot(queries, all_keys.T, preferred_element_type=jnp.float32) * scale + q_bias
    score = jnp.where(q_allowed, score, jnp.float32(NEG))
    top = jnp.max(score, axis=-1)
    expo = jnp.where(q_allowed, jnp.exp(score - top[:, None]), jnp.float32(0.0))
    total = jnp.sum(expo, axis=-1)
    out = jnp.dot(expo.astype(jnp.bfloat16), all_values, preferred_element_type=jnp.float32)
    out = (out / total[:, None]).astype(jnp.bfloat16)
    lse = top + jnp.log(total)
    delta = jnp.sum(d_out.astype(jnp.float32) * out.astype(jnp.float32), axis=-1)
    prob = jnp.where(q_allowed, jnp.exp(score - lse[:, None]), jnp.float32(0.0))
    dprob = jnp.dot(d_out, all_values.T, preferred_element_type=jnp.float32)
    dscore = (prob * (dprob - delta[:, None])).astype(jnp.bfloat16)
    d_query = jnp.dot(dscore, all_keys, preferred_element_type=jnp.float32) * scale

    stats = jnp.take(xor_gather(jnp.stack([lse, delta], axis=0), ("zh", "y", "core")), owner, axis=0)
    all_lse = stats[:, 0].reshape(total_rows)
    all_delta = stats[:, 1].reshape(total_rows)

    all_rows = jnp.dot(all_block.astype(jnp.bfloat16), mask_b).astype(jnp.bfloat16)
    k_open = jnp.dot(all_rows, own_block.T.astype(jnp.bfloat16), preferred_element_type=jnp.float32) > 0.5
    k_allowed = (own_pos[None, :] <= pos[:, None]) & (
        k_open | (own_pos[None, :] // BLK == pos[:, None] // BLK)
    )
    k_bias = jnp.dot(all_onehot, jnp.take(table.T, roles, axis=0).T, precision=HI)
    score_t = jnp.dot(all_queries, own_keys.T, preferred_element_type=jnp.float32) * scale + k_bias
    prob_t = jnp.where(k_allowed, jnp.exp(score_t - all_lse[:, None]), jnp.float32(0.0))
    dprob_t = jnp.dot(all_grads, own_values.T, preferred_element_type=jnp.float32)
    dscore_t = (prob_t * (dprob_t - all_delta[:, None])).astype(jnp.bfloat16)
    d_key = jnp.dot(dscore_t.T, all_queries, preferred_element_type=jnp.float32) * scale
    d_value = jnp.dot(prob_t.astype(jnp.bfloat16).T, all_grads, preferred_element_type=jnp.float32)

    partial = shifted_all(jnp.stack([d_key, d_value], axis=0), "x")
    kv_sum = partial[0]
    for k in range(1, partial.shape[0]):
        kv_sum = kv_sum + partial[k]
    kv_all = shifted_all(kv_sum.astype(jnp.bfloat16), "g")
    kv_all = kv_all.transpose(1, 2, 0, 3).reshape(2, rows, -1)
    return (out, d_query.astype(jnp.bfloat16), kv_all[0], kv_all[1])


def solution(mesh):
    ctx_size = mesh.shape["ctx"]
    tp_size = mesh.shape["tp"]
    devices = np.asarray(mesh.devices).reshape(ctx_size, tp_size // GROUP, GROUP)
    inner = Mesh(devices.reshape(2, ctx_size // 4, 2, tp_size // GROUP, GROUP), ("zh", "y", "core", "g", "x"))
    heads = ("g", "x")
    seq = ("zh", "y", "core")
    return jax.shard_map(
        on_device,
        mesh=inner,
        in_specs=(
            P(seq, heads),
            P(seq, None),
            P(seq, None),
            P(seq),
            P(heads, None, None),
            P(),
            P(seq, heads),
        ),
        out_specs=(P(seq, heads), P(seq, heads), P(seq, None), P(seq, None)),
        check_vma=False,
    )
```

```python
import math

import jax
import jax.numpy as jnp
import numpy as np
from jax import lax
from jax.sharding import Mesh
from jax.sharding import PartitionSpec as P

HS = 128
GROUP = 4
BLK = 128
NEG = -1e30
HI = lax.Precision.HIGHEST


def xor_pairs(count, bit):
    return [(i, i ^ bit) for i in range(count)]


def xor_gather(block, axis):
    count = lax.axis_size(axis)
    me = lax.axis_index(axis)
    held = block[None]
    bit = 1
    while bit < count:
        held = jnp.concatenate([held, lax.ppermute(held, axis, xor_pairs(count, bit))], axis=0)
        bit *= 2
    return jnp.take(held, me ^ jnp.arange(count), axis=0)


def xor_sum(value, axis):
    count = lax.axis_size(axis)
    bit = 1
    while bit < count:
        value = value + lax.ppermute(value, axis, xor_pairs(count, bit))
        bit *= 2
    return value


def bruck_gather(block, axis):
    count = lax.axis_size(axis)
    me = lax.axis_index(axis)
    held = block[None]
    step = 1
    while step < count:
        part = held[: min(step, count - step)]
        pairs = [(i, (i - step) % count) for i in range(count)]
        held = jnp.concatenate([held, lax.ppermute(part, axis, pairs)], axis=0)
        step *= 2
    return jnp.take(held, (jnp.arange(count) - me) % count, axis=0)


def shift_pairs(count, step):
    return [(i, (i + step) % count) for i in range(count)]


def gather_ctx(full, half):
    zh = lax.axis_index("zh")
    y = lax.axis_index("y")
    core = lax.axis_index("core")
    ny = lax.axis_size("y")
    ncore = lax.axis_size("core")
    nz = lax.axis_size("zh")

    def index_of(z, yy, cc):
        return (z * ny + yy) * ncore + cc

    chip = jnp.concatenate([full, lax.ppermute(half, "zh", xor_pairs(nz, 1))], axis=0)[None]
    blocks = [chip]
    owners = [jnp.stack([index_of(zh, y, core), index_of(1 - zh, y, core)])]
    left = chip
    right = chip
    for step in range(1, ny // 2 + 1):
        left = lax.ppermute(left, "y", shift_pairs(ny, 1))
        blocks.append(left)
        yy = (y - step) % ny
        owners.append(jnp.stack([index_of(zh, yy, core), index_of(1 - zh, yy, core)]))
        if step < ny - step:
            right = lax.ppermute(right, "y", shift_pairs(ny, -1))
            blocks.append(right)
            yy = (y + step) % ny
            owners.append(jnp.stack([index_of(zh, yy, core), index_of(1 - zh, yy, core)]))
    mine = jnp.concatenate(blocks, axis=0)
    owner = jnp.stack(owners)
    other = lax.ppermute(mine, "core", xor_pairs(ncore, 1))
    every = jnp.concatenate([mine, other], axis=0)
    owner = jnp.concatenate([owner, owner - core + (1 - core)], axis=0)
    rows = full.shape[0]
    return every[:, :rows], every[:, rows:], owner[:, 0], owner[:, 1]


def shifted_all(value, axis):
    count = lax.axis_size(axis)
    me = lax.axis_index(axis)
    parts = [value] + [lax.ppermute(value, axis, shift_pairs(count, s)) for s in range(1, count)]
    ordered = []
    for k in range(count):
        source = (me - k) % count
        chosen = parts[0]
        for s in range(1, count):
            chosen = jnp.where(source == s, parts[s], chosen)
        ordered.append(chosen)
    return ordered


def on_device(queries, keys, values, roles, role_table, block_mask, d_out):
    rows = queries.shape[0]
    role_count = role_table.shape[1]
    scale = 1.0 / math.sqrt(HS)
    ctx_index = (lax.axis_index("zh") * lax.axis_size("y") + lax.axis_index("y")) * lax.axis_size(
        "core"
    ) + lax.axis_index("core")
    group = lax.axis_index("g")
    own_keys = lax.dynamic_slice_in_dim(keys, group * HS, HS, 1)
    own_values = lax.dynamic_slice_in_dim(values, group * HS, HS, 1)
    table = role_table[0]

    role_onehot = (roles[:, None] == jnp.arange(role_count)[None, :]).astype(jnp.float32)
    role_rows = jnp.zeros((16, rows), jnp.bfloat16).at[0].set(roles.astype(jnp.bfloat16))
    packed = jnp.concatenate([own_keys, own_values, queries, d_out, role_rows], axis=0)
    early = lax.axis_index("zh") == 0
    half = jnp.concatenate(
        [jnp.where(early, own_keys, queries), jnp.where(early, own_values, d_out), role_rows], axis=0
    )
    near, far, near_owner, far_owner = gather_ctx(packed, half)
    owner = jnp.concatenate([near_owner, far_owner])
    total_rows = 2 * near.shape[0] * rows

    def joined(near_part, far_part):
        return jnp.concatenate([near_part, far_part], axis=0).reshape((total_rows,) + near_part.shape[2:])

    all_keys = joined(near[:, 0:rows], far[:, 0:rows])
    all_values = joined(near[:, rows : 2 * rows], far[:, rows : 2 * rows])
    all_queries = joined(near[:, 2 * rows : 3 * rows], far[:, 0:rows])
    all_grads = joined(near[:, 3 * rows : 4 * rows], far[:, rows : 2 * rows])
    all_roles = joined(near[:, 4 * rows], far[:, 2 * rows]).astype(jnp.int32)
    all_onehot = (all_roles[:, None] == jnp.arange(role_count)[None, :]).astype(jnp.float32)

    pos = (owner[:, None] * rows + jnp.arange(rows)[None, :]).reshape(total_rows)
    own_pos = ctx_index * rows + jnp.arange(rows)
    mask_f = block_mask.astype(jnp.float32)
    all_block = (pos[:, None] // BLK == jnp.arange(block_mask.shape[0])[None, :]).astype(jnp.float32)
    own_block = (own_pos[:, None] // BLK == jnp.arange(block_mask.shape[0])[None, :]).astype(jnp.float32)

    q_open = jnp.dot(jnp.dot(own_block, mask_f, precision=HI), all_block.T, precision=HI) > 0.5
    q_allowed = (pos[None, :] <= own_pos[:, None]) & (
        q_open | (pos[None, :] // BLK == own_pos[:, None] // BLK)
    )
    q_bias = jnp.dot(jnp.dot(role_onehot, table, precision=HI), all_onehot.T, precision=HI)
    score = jnp.dot(queries, all_keys.T, preferred_element_type=jnp.float32) * scale + q_bias
    score = jnp.where(q_allowed, score, jnp.float32(NEG))
    top = jnp.max(score, axis=-1)
    expo = jnp.where(q_allowed, jnp.exp(score - top[:, None]), jnp.float32(0.0))
    total = jnp.sum(expo, axis=-1)
    out = jnp.dot(expo.astype(jnp.bfloat16), all_values, preferred_element_type=jnp.float32)
    out = (out / total[:, None]).astype(jnp.bfloat16)
    lse = top + jnp.log(total)
    delta = jnp.sum(d_out.astype(jnp.float32) * out.astype(jnp.float32), axis=-1)
    prob = jnp.where(q_allowed, jnp.exp(score - lse[:, None]), jnp.float32(0.0))
    dprob = jnp.dot(d_out, all_values.T, preferred_element_type=jnp.float32)
    dscore = (prob * (dprob - delta[:, None])).astype(jnp.bfloat16)
    d_query = jnp.dot(dscore, all_keys, preferred_element_type=jnp.float32) * scale

    stats = jnp.take(xor_gather(jnp.stack([lse, delta], axis=0), ("zh", "y", "core")), owner, axis=0)
    all_lse = stats[:, 0].reshape(total_rows)
    all_delta = stats[:, 1].reshape(total_rows)

    k_open = jnp.dot(jnp.dot(all_block, mask_f, precision=HI), own_block.T, precision=HI) > 0.5
    k_allowed = (own_pos[None, :] <= pos[:, None]) & (
        k_open | (own_pos[None, :] // BLK == pos[:, None] // BLK)
    )
    k_bias = jnp.dot(all_onehot, jnp.dot(table, role_onehot.T, precision=HI), precision=HI)
    score_t = jnp.dot(all_queries, own_keys.T, preferred_element_type=jnp.float32) * scale + k_bias
    prob_t = jnp.where(k_allowed, jnp.exp(score_t - all_lse[:, None]), jnp.float32(0.0))
    dprob_t = jnp.dot(all_grads, own_values.T, preferred_element_type=jnp.float32)
    dscore_t = (prob_t * (dprob_t - all_delta[:, None])).astype(jnp.bfloat16)
    d_key = jnp.dot(dscore_t.T, all_queries, preferred_element_type=jnp.float32) * scale
    d_value = jnp.dot(prob_t.astype(jnp.bfloat16).T, all_grads, preferred_element_type=jnp.float32)

    partial = shifted_all(jnp.stack([d_key, d_value], axis=0), "x")
    kv_sum = partial[0]
    for k in range(1, len(partial)):
        kv_sum = kv_sum + partial[k]
    kv_all = jnp.concatenate(shifted_all(kv_sum.astype(jnp.bfloat16), "g"), axis=-1)
    return (out, d_query.astype(jnp.bfloat16), kv_all[0], kv_all[1])


def solution(mesh):
    ctx_size = mesh.shape["ctx"]
    tp_size = mesh.shape["tp"]
    devices = np.asarray(mesh.devices).reshape(ctx_size, tp_size // GROUP, GROUP)
    inner = Mesh(devices.reshape(2, ctx_size // 4, 2, tp_size // GROUP, GROUP), ("zh", "y", "core", "g", "x"))
    heads = ("g", "x")
    seq = ("zh", "y", "core")
    return jax.shard_map(
        on_device,
        mesh=inner,
        in_specs=(
            P(seq, heads),
            P(seq, None),
            P(seq, None),
            P(seq),
            P(heads, None, None),
            P(),
            P(seq, heads),
        ),
        out_specs=(P(seq, heads), P(seq, heads), P(seq, None), P(seq, None)),
        check_vma=False,
    )
```

```python
import math

import jax
import jax.numpy as jnp
import numpy as np
from jax import lax
from jax.sharding import Mesh
from jax.sharding import PartitionSpec as P

HS = 128
GROUP = 4
BLK = 128
NEG = -1e30
HI = lax.Precision.HIGHEST


def xor_pairs(count, bit):
    return [(i, i ^ bit) for i in range(count)]


def xor_gather(block, axis):
    count = lax.axis_size(axis)
    me = lax.axis_index(axis)
    held = block[None]
    bit = 1
    while bit < count:
        held = jnp.concatenate([held, lax.ppermute(held, axis, xor_pairs(count, bit))], axis=0)
        bit *= 2
    return held


def xor_sum(value, axis):
    count = lax.axis_size(axis)
    bit = 1
    while bit < count:
        value = value + lax.ppermute(value, axis, xor_pairs(count, bit))
        bit *= 2
    return value


def bruck_gather(block, axis):
    count = lax.axis_size(axis)
    me = lax.axis_index(axis)
    held = block[None]
    step = 1
    while step < count:
        part = held[: min(step, count - step)]
        pairs = [(i, (i - step) % count) for i in range(count)]
        held = jnp.concatenate([held, lax.ppermute(part, axis, pairs)], axis=0)
        step *= 2
    return jnp.take(held, (jnp.arange(count) - me) % count, axis=0)


def shift_pairs(count, step):
    return [(i, (i + step) % count) for i in range(count)]


def gather_ctx(full, half):
    zh = lax.axis_index("zh")
    y = lax.axis_index("y")
    core = lax.axis_index("core")
    ny = lax.axis_size("y")
    ncore = lax.axis_size("core")
    nz = lax.axis_size("zh")

    def index_of(z, yy, cc):
        return (z * ny + yy) * ncore + cc

    chip = jnp.concatenate([full, lax.ppermute(half, "zh", xor_pairs(nz, 1))], axis=0)[None]
    blocks = [chip]
    owners = [jnp.stack([index_of(zh, y, core), index_of(1 - zh, y, core)])]
    left = chip
    right = chip
    for step in range(1, ny // 2 + 1):
        left = lax.ppermute(left, "y", shift_pairs(ny, 1))
        blocks.append(left)
        yy = (y - step) % ny
        owners.append(jnp.stack([index_of(zh, yy, core), index_of(1 - zh, yy, core)]))
        if step < ny - step:
            right = lax.ppermute(right, "y", shift_pairs(ny, -1))
            blocks.append(right)
            yy = (y + step) % ny
            owners.append(jnp.stack([index_of(zh, yy, core), index_of(1 - zh, yy, core)]))
    mine = jnp.concatenate(blocks, axis=0)
    owner = jnp.stack(owners)
    other = lax.ppermute(mine, "core", xor_pairs(ncore, 1))
    every = jnp.concatenate([mine, other], axis=0)
    owner = jnp.concatenate([owner, owner - core + (1 - core)], axis=0)
    rows = full.shape[0]
    return every[:, :rows], every[:, rows:], owner[:, 0], owner[:, 1]


def shifted_all(value, axis):
    count = lax.axis_size(axis)
    me = lax.axis_index(axis)
    parts = [value] + [lax.ppermute(value, axis, shift_pairs(count, s)) for s in range(1, count)]
    ordered = []
    for k in range(count):
        source = (me - k) % count
        chosen = parts[0]
        for s in range(1, count):
            chosen = jnp.where(source == s, parts[s], chosen)
        ordered.append(chosen)
    return ordered


def on_device(queries, keys, values, roles, role_table, block_mask, d_out):
    rows = queries.shape[0]
    role_count = role_table.shape[1]
    scale = 1.0 / math.sqrt(HS)
    ctx_index = (lax.axis_index("zh") * lax.axis_size("y") + lax.axis_index("y")) * lax.axis_size(
        "core"
    ) + lax.axis_index("core")
    group = lax.axis_index("g")
    own_keys = lax.dynamic_slice_in_dim(keys, group * HS, HS, 1)
    own_values = lax.dynamic_slice_in_dim(values, group * HS, HS, 1)
    table = role_table[0]

    role_onehot = (roles[:, None] == jnp.arange(role_count)[None, :]).astype(jnp.float32)
    role_rows = jnp.zeros((16, rows), jnp.bfloat16).at[0].set(roles.astype(jnp.bfloat16))
    packed = jnp.concatenate([own_keys, own_values, queries, d_out, role_rows], axis=0)
    early = lax.axis_index("zh") == 0
    half = jnp.concatenate(
        [jnp.where(early, own_keys, queries), jnp.where(early, own_values, d_out), role_rows], axis=0
    )
    near, far, near_owner, far_owner = gather_ctx(packed, half)
    owner = jnp.concatenate([near_owner, far_owner])
    total_rows = 2 * near.shape[0] * rows

    def joined(near_part, far_part):
        return jnp.concatenate([near_part, far_part], axis=0).reshape((total_rows,) + near_part.shape[2:])

    all_keys = joined(near[:, 0:rows], far[:, 0:rows])
    all_values = joined(near[:, rows : 2 * rows], far[:, rows : 2 * rows])
    all_queries = joined(near[:, 2 * rows : 3 * rows], far[:, 0:rows])
    all_grads = joined(near[:, 3 * rows : 4 * rows], far[:, rows : 2 * rows])
    all_roles = joined(near[:, 4 * rows], far[:, 2 * rows]).astype(jnp.int32)
    all_onehot = (all_roles[:, None] == jnp.arange(role_count)[None, :]).astype(jnp.float32)

    pos = (owner[:, None] * rows + jnp.arange(rows)[None, :]).reshape(total_rows)
    own_pos = ctx_index * rows + jnp.arange(rows)
    mask_f = block_mask.astype(jnp.float32)
    all_block = (pos[:, None] // BLK == jnp.arange(block_mask.shape[0])[None, :]).astype(jnp.float32)
    own_block = (own_pos[:, None] // BLK == jnp.arange(block_mask.shape[0])[None, :]).astype(jnp.float32)

    q_open = jnp.dot(jnp.dot(own_block, mask_f, precision=HI), all_block.T, precision=HI) > 0.5
    q_allowed = (pos[None, :] <= own_pos[:, None]) & (
        q_open | (pos[None, :] // BLK == own_pos[:, None] // BLK)
    )
    q_bias = jnp.dot(jnp.dot(role_onehot, table, precision=HI), all_onehot.T, precision=HI)
    score = jnp.dot(queries, all_keys.T, preferred_element_type=jnp.float32) * scale + q_bias
    score = jnp.where(q_allowed, score, jnp.float32(NEG))
    top = jnp.max(score, axis=-1)
    expo = jnp.where(q_allowed, jnp.exp(score - top[:, None]), jnp.float32(0.0))
    total = jnp.sum(expo, axis=-1)
    out = jnp.dot(expo.astype(jnp.bfloat16), all_values, preferred_element_type=jnp.float32)
    out = (out / total[:, None]).astype(jnp.bfloat16)
    lse = top + jnp.log(total)
    delta = jnp.sum(d_out.astype(jnp.float32) * out.astype(jnp.float32), axis=-1)
    prob = jnp.where(q_allowed, jnp.exp(score - lse[:, None]), jnp.float32(0.0))
    dprob = jnp.dot(d_out, all_values.T, preferred_element_type=jnp.float32)
    dscore = (prob * (dprob - delta[:, None])).astype(jnp.bfloat16)
    d_query = jnp.dot(dscore, all_keys, preferred_element_type=jnp.float32) * scale

    stats = jnp.take(xor_gather(jnp.stack([lse, delta], axis=0), ("zh", "y", "core")), owner ^ ctx_index, axis=0)
    all_lse = stats[:, 0].reshape(total_rows)
    all_delta = stats[:, 1].reshape(total_rows)

    k_open = jnp.dot(jnp.dot(all_block, mask_f, precision=HI), own_block.T, precision=HI) > 0.5
    k_allowed = (own_pos[None, :] <= pos[:, None]) & (
        k_open | (own_pos[None, :] // BLK == pos[:, None] // BLK)
    )
    k_bias = jnp.dot(all_onehot, jnp.dot(table, role_onehot.T, precision=HI), precision=HI)
    score_t = jnp.dot(all_queries, own_keys.T, preferred_element_type=jnp.float32) * scale + k_bias
    prob_t = jnp.where(k_allowed, jnp.exp(score_t - all_lse[:, None]), jnp.float32(0.0))
    dprob_t = jnp.dot(all_grads, own_values.T, preferred_element_type=jnp.float32)
    dscore_t = (prob_t * (dprob_t - all_delta[:, None])).astype(jnp.bfloat16)
    d_key = jnp.dot(dscore_t.T, all_queries, preferred_element_type=jnp.float32) * scale
    d_value = jnp.dot(prob_t.astype(jnp.bfloat16).T, all_grads, preferred_element_type=jnp.float32)

    partial = shifted_all(jnp.stack([d_key, d_value], axis=0), "x")
    kv_sum = partial[0]
    for k in range(1, len(partial)):
        kv_sum = kv_sum + partial[k]
    kv_all = jnp.concatenate(shifted_all(kv_sum.astype(jnp.bfloat16), "g"), axis=-1)
    return (out, d_query.astype(jnp.bfloat16), kv_all[0], kv_all[1])


def solution(mesh):
    ctx_size = mesh.shape["ctx"]
    tp_size = mesh.shape["tp"]
    devices = np.asarray(mesh.devices).reshape(ctx_size, tp_size // GROUP, GROUP)
    inner = Mesh(devices.reshape(2, ctx_size // 4, 2, tp_size // GROUP, GROUP), ("zh", "y", "core", "g", "x"))
    heads = ("g", "x")
    seq = ("zh", "y", "core")
    return jax.shard_map(
        on_device,
        mesh=inner,
        in_specs=(
            P(seq, heads),
            P(seq, None),
            P(seq, None),
            P(seq),
            P(heads, None, None),
            P(),
            P(seq, heads),
        ),
        out_specs=(P(seq, heads), P(seq, heads), P(seq, None), P(seq, None)),
        check_vma=False,
    )
```
